512 devices in a mesh: ctx: 64 (over z, x), ch: 8 (over y, core).
Axes of the slice: x: 4, y: 4, z: 16, core: 2. Of those that a mesh axis runs over, the one named last changes fastest.
Arguments:
- query: bfloat16 [8192, 4096], P('ctx', 'ch'), may hold values from -6 to 6
- key: bfloat16 [8192, 4096], P('ctx', 'ch'), may hold values from -6 to 6
- value: bfloat16 [8192, 4096], P('ctx', 'ch'), may hold values from -6 to 6
- filter_taps: float32 [8192, 256], P('ctx', 'ch'), may hold values from -0.0625 to 0.0625
- conv_bias: float32 [4096], P('ch'), may hold values from -4 to 4
- norm_gain: float32 [4096], P('ch'), may hold values from 0.1 to 1.9
- pair_list: int32 [2080, 3], replicated, may hold values from 0 to 63, as said below
Outputs:
- mixed: bfloat16 [8192, 4096], P('ctx', 'ch')
The draws below stay inside these ranges and needn't reach their ends.
Inputs may be any that keep to these rules, and one draw needn't show every extreme that they name: `pair_list`: every pair of blocks with source <= target appears once, in no particular order. A row with source = target names the device that holds that block; blocks c and 63 - c are held by two devices whose indices differ only in the lowest bit. Every other pair is executed by one of those two devices for its target block. Each device executes at most 33 pairs.
All inputs are finite; a program needn't handle non-finite values.
Results may differ from the reference program's by a relative error of at most 0.0049.
Values may be sent and summed in bfloat16 or wider, within the bound.
No kernel may reach another device: no remote copies, remote signals or barrier semaphores. Data moves between devices by JAX's collectives and lax.ppermute only.
A program may use at most 64 MiB of HBM per device.

```python
import jax
import jax.numpy as jnp
import numpy as np
from jax import lax

SPAN = 128
CHANNELS = 4096
GROUP = 16
FILTERS = 256
SEQ = 8192


def draw_pair_list(key, part):
    blocks = SEQ // SPAN
    half_count = blocks // 2
    pair_perm = jax.random.permutation(jax.random.fold_in(key, 1), half_count).astype(jnp.int32)
    flipped = jax.random.randint(jax.random.fold_in(key, 2), (half_count,), 0, 2).astype(jnp.int32)
    short_dev = 2 * pair_perm + flipped
    long_dev = 2 * pair_perm + 1 - flipped
    row_keys = jax.random.split(jax.random.fold_in(key, 3), half_count)
    scores = jax.vmap(lambda k: jax.random.permutation(k, blocks))(row_keys).astype(jnp.int32)
    row_ids = jnp.arange(half_count, dtype=jnp.int32)[:, None]
    sources = jnp.arange(blocks, dtype=jnp.int32)[None, :]
    eligible = sources <= blocks - 2 - row_ids
    smaller = eligible[:, None, :] & (scores[:, None, :] < scores[:, :, None])
    ranked = jnp.sum(smaller.astype(jnp.int32), axis=2)
    chosen = eligible & (ranked < half_count - row_ids)
    target_np, source_np = np.tril_indices(blocks)
    target_all = jnp.asarray(target_np.astype(np.int32))
    source_all = jnp.asarray(source_np.astype(np.int32))
    row_pair = jnp.minimum(target_all, blocks - 1 - target_all)
    is_short = target_all < half_count
    picked = chosen[row_pair, source_all]
    runner = jnp.where(is_short | picked, short_dev[row_pair], long_dev[row_pair])
    rows = jnp.stack([source_all, target_all, runner.astype(jnp.int32)], axis=1).astype(jnp.int32)
    shuffle = jax.random.permutation(jax.random.fold_in(key, 4), rows.shape[0])
    return rows[shuffle]


def level_of(rng, dims, shards, least, largest):
    def one(axis_at, shards_of):
        heights = jax.random.uniform(jax.random.fold_in(jax.random.fold_in(rng, 6), axis_at), (shards_of,), jnp.float32, least / len(shards), largest / len(shards))
        return jnp.repeat(jnp.exp(heights), dims[axis_at] // shards_of).reshape((-1,) + (1,) * (len(dims) - axis_at - 1))

    factor_of = one(*shards[0])
    for cut in shards[1:]:
        factor_of = factor_of * one(*cut)
    return factor_of


def gaussian(key, extent, scale, most, pieces=(), held_as=jnp.bfloat16):
    result = scale * jax.random.normal(key, extent, jnp.float32)
    if pieces:
        result = result * level_of(key, extent, pieces, -0.22, 0.18)
    return jnp.clip(result, -most, most).astype(held_as)


def setup_inputs(seed: int = 0) -> dict:
    seeds = jax.random.split(jax.random.key(seed), 8)
    return {
        "query": gaussian(seeds[0], (SEQ, CHANNELS), 1.0, 6.0, ((0, 64), (1, 8))),
        "key": gaussian(seeds[1], (SEQ, CHANNELS), 1.0, 6.0, ((0, 64), (1, 8))),
        "value": gaussian(seeds[2], (SEQ, CHANNELS), 1.0, 6.0, ((0, 64), (1, 8))),
        "filter_taps": gaussian(seeds[3], (SEQ, FILTERS), SEQ ** -0.5, 0.0625, ((0, 64), (1, 8)), jnp.float32),
        "conv_bias": gaussian(seeds[4], (CHANNELS,), 1.0, 4.0, ((0, 8),), jnp.float32),
        "norm_gain": jnp.clip(1.0 + 0.18 * jax.random.normal(seeds[5], (CHANNELS,), jnp.float32), 0.1, 1.9),
        "pair_list": draw_pair_list(jax.random.fold_in(seeds[7], 71), 0),
    }


def reference(query, key, value, filter_taps, conv_bias, norm_gain, pair_list):
    blocks = SEQ // SPAN
    source = pair_list[:, 0]
    target = pair_list[:, 1]
    runner = pair_list[:, 2]
    on_diag = source == target
    slots = jnp.arange(blocks, dtype=jnp.int32)
    holds = on_diag[:, None] & (runner[:, None] == slots[None, :])
    holder = lax.optimization_barrier(jnp.sum(jnp.where(holds, source[:, None], 0), axis=0)).astype(jnp.int32)
    keeps = on_diag[:, None] & (source[:, None] == slots[None, :])
    device_of = lax.optimization_barrier(jnp.sum(jnp.where(keeps, runner[:, None], 0), axis=0)).astype(jnp.int32)
    signal = (key.astype(jnp.float32) * value.astype(jnp.float32)).astype(jnp.bfloat16)
    ordered = signal.astype(jnp.float32).reshape(blocks, SPAN, CHANNELS)[device_of].reshape(SEQ, CHANNELS)
    taps = jnp.repeat(filter_taps, GROUP, axis=1)
    length = 2 * SEQ
    spectrum = jnp.fft.rfft(ordered, n=length, axis=0) * jnp.fft.rfft(taps, n=length, axis=0)
    long_conv = jnp.fft.irfft(spectrum, n=length, axis=0)[:SEQ]
    long_conv = long_conv + conv_bias[None, :] * ordered
    placed = long_conv.reshape(blocks, SPAN, CHANNELS)[holder].reshape(SEQ, CHANNELS)
    gated = query.astype(jnp.float32) * placed
    meansq = lax.optimization_barrier(jnp.mean(gated * gated, axis=1, keepdims=True))
    return (gated * lax.rsqrt(meansq + 1e-05) * norm_gain[None, :]).astype(jnp.bfloat16)
```

```python
import jax
import jax.numpy as jnp
from jax import lax
from jax.sharding import PartitionSpec as P


def placement(pair_list, blocks):
    source = pair_list[:, 0]
    target = pair_list[:, 1]
    runner = pair_list[:, 2]
    slots = lax.iota(jnp.int32, blocks)
    on_diag = source == target
    holds = on_diag[:, None] & (runner[:, None] == slots[None, :])
    holder = jnp.sum(jnp.where(holds, source[:, None], 0), axis=0)
    keeps = on_diag[:, None] & (source[:, None] == slots[None, :])
    device_of = jnp.sum(jnp.where(keeps, runner[:, None], 0), axis=0)
    return holder, device_of


def toeplitz_rows(taps, blocks, rows):
    lag_blocks = taps.reshape(blocks, rows)
    earlier = jnp.concatenate([jnp.zeros((1, rows), taps.dtype), lag_blocks[:-1]], axis=0)
    window = jnp.concatenate([earlier, lag_blocks], axis=1)[:, ::-1]
    table = jnp.stack(
        [window[:, rows - 1 - i : 2 * rows - 1 - i] for i in range(rows)], axis=0
    )
    return table.reshape(rows, blocks * rows)


def body(query, key, value, filter_taps, conv_bias, norm_gain, pair_list):
    rows = query.shape[0]
    channels = query.shape[1]
    groups = filter_taps.shape[1]
    blocks = lax.axis_size("ctx")
    width = channels // blocks
    share = (channels // groups) // width
    holder, device_of = placement(pair_list, blocks)

    signal = (key.astype(jnp.float32) * value.astype(jnp.float32)).astype(jnp.bfloat16)

    spread_taps = jnp.repeat(filter_taps, share, axis=1)
    my_taps = lax.all_to_all(spread_taps, "ctx", 1, 0, tiled=True)[:, 0]
    table = toeplitz_rows(my_taps, blocks, rows)
    table_hi = table.astype(jnp.bfloat16)
    table_lo = (table - table_hi.astype(jnp.float32)).astype(jnp.bfloat16)

    gathered = lax.all_to_all(signal, "ctx", 1, 0, tiled=True)
    in_order = gathered.reshape(blocks, rows, width)[device_of]
    padded = jnp.concatenate([jnp.zeros_like(in_order), in_order], axis=0)
    shifted = jnp.stack(
        [padded[blocks - lag : 2 * blocks - lag] for lag in range(blocks)], axis=0
    )
    shifted = shifted.transpose(0, 2, 1, 3).reshape(blocks * rows, blocks * width)

    conv = jnp.dot(table_hi, shifted, preferred_element_type=jnp.float32)
    conv = conv + jnp.dot(table_lo, shifted, preferred_element_type=jnp.float32)
    conv = conv.reshape(rows, blocks, width)[:, holder, :]
    conv = lax.all_to_all(conv, "ctx", 1, 1, tiled=True).reshape(rows, channels)

    long_conv = conv + conv_bias[None, :] * signal.astype(jnp.float32)
    gated = query.astype(jnp.float32) * long_conv
    squares = jnp.sum(gated * gated, axis=1)
    total_sq = lax.psum(squares, "ch")
    scaling = lax.rsqrt(total_sq / (channels * lax.axis_size("ch")) + 1e-05)
    return (gated * scaling[:, None] * norm_gain[None, :]).astype(jnp.bfloat16)


def solution(mesh):
    placed = (P("ctx", "ch"), P("ctx", "ch"), P("ctx", "ch"), P("ctx", "ch"), P("ch"), P("ch"), P())
    return jax.shard_map(
        body, mesh=mesh, in_specs=placed, out_specs=P("ctx", "ch"), check_vma=False
    )
```

```python
import jax
import jax.numpy as jnp
from jax import lax
from jax.experimental import pallas as pl
from jax.experimental.pallas import tpu as pltpu
from jax.sharding import PartitionSpec as P


def placement(pair_list, blocks):
    source = pair_list[:, 0]
    target = pair_list[:, 1]
    runner = pair_list[:, 2]
    slots = lax.iota(jnp.int32, blocks)
    on_diag = source == target
    holds = on_diag[:, None] & (runner[:, None] == slots[None, :])
    holder = jnp.sum(jnp.where(holds, source[:, None], 0), axis=0)
    keeps = on_diag[:, None] & (source[:, None] == slots[None, :])
    device_of = jnp.sum(jnp.where(keeps, runner[:, None], 0), axis=0)
    return holder, device_of


def to_bf16_grid(values):
    return lax.reduce_precision(values, exponent_bits=8, mantissa_bits=7)


def conv_kernel(width, window_ref, signal_ref, out_ref):
    rows = out_ref.shape[0]
    lanes = out_ref.shape[1]
    blocks = window_ref.shape[0]
    signal = signal_ref[...].astype(jnp.float32)
    lane = lax.broadcasted_iota(jnp.int32, (rows, lanes), 1)

    def step(lag, total):
        window = jnp.broadcast_to(window_ref[pl.ds(lag, 1), :], (rows, 2 * rows))
        skewed = pltpu.roll(window, rows + 1, 1, stride=1, stride_axis=0)
        block = skewed[:, :rows]
        block_hi = block.astype(jnp.bfloat16)
        block_lo = (block - block_hi.astype(jnp.float32)).astype(jnp.bfloat16)
        moved = pltpu.roll(signal, lag * width, 1)
        moved = jnp.where(lane >= lag * width, moved, 0.0).astype(jnp.bfloat16)
        total = total + jnp.dot(block_hi, moved, preferred_element_type=jnp.float32)
        total = total + jnp.dot(block_lo, moved, preferred_element_type=jnp.float32)
        return total

    out_ref[...] = lax.fori_loop(
        0, blocks, step, jnp.zeros((rows, lanes), jnp.float32), unroll=2
    )


def causal_conv(window, signal, width):
    rows, lanes = signal.shape
    blocks = window.shape[0]
    return pl.pallas_call(
        lambda *refs: conv_kernel(width, *refs),
        out_shape=jax.ShapeDtypeStruct((rows, lanes), jnp.float32),
        in_specs=[pl.BlockSpec(memory_space=pltpu.VMEM)] * 2,
        out_specs=pl.BlockSpec(memory_space=pltpu.VMEM),
        cost_estimate=pl.CostEstimate(
            flops=4 * rows * rows * lanes * blocks,
            bytes_accessed=window.size * 4 + signal.size * 2 + rows * lanes * 4,
            transcendentals=0,
        ),
    )(window, signal)


def body(query, key, value, filter_taps, conv_bias, norm_gain, pair_list):
    rows = query.shape[0]
    channels = query.shape[1]
    groups = filter_taps.shape[1]
    blocks = lax.axis_size("ctx")
    width = channels // blocks
    share = (channels // groups) // width
    holder, device_of = placement(pair_list, blocks)

    product = to_bf16_grid(key.astype(jnp.float32) * value.astype(jnp.float32))
    signal = product.astype(jnp.bfloat16)

    taps_hi = to_bf16_grid(filter_taps)
    taps_lo = filter_taps - taps_hi
    coded = jnp.stack([taps_hi.T, taps_lo.T], axis=1).reshape(groups, 2, rows // width, width)
    coded = jnp.repeat(coded, share, axis=0).reshape(blocks, 2 * rows // width, width)
    coded = coded.transpose(1, 0, 2).reshape(2 * rows // width, channels)
    outgoing = jnp.concatenate([signal, coded.astype(jnp.bfloat16)], axis=0)

    incoming = lax.all_to_all(outgoing, "ctx", 1, 0, tiled=True)
    incoming = incoming.reshape(blocks, rows + 2 * rows // width, width)
    in_order = incoming[:, :rows, :][device_of]
    taps_in = incoming[:, rows:, :].astype(jnp.float32).reshape(blocks, 2, rows)
    my_taps = taps_in[:, 0, :] + taps_in[:, 1, :]
    earlier = jnp.concatenate([jnp.zeros((1, rows), jnp.float32), my_taps[:-1]], axis=0)
    window = jnp.concatenate([earlier, my_taps], axis=1)[:, ::-1]

    lined = in_order.transpose(1, 0, 2).reshape(rows, blocks * width)
    conv = causal_conv(window, lined, width)
    conv = conv.reshape(rows, blocks, width)[:, holder, :]
    conv = lax.all_to_all(conv, "ctx", 1, 1, tiled=True).reshape(rows, channels)

    long_conv = conv + conv_bias[None, :] * product
    gated = query.astype(jnp.float32) * long_conv
    squares = jnp.sum(gated * gated, axis=1)
    total_sq = lax.psum(squares, "ch")
    scaling = lax.rsqrt(total_sq / (channels * lax.axis_size("ch")) + 1e-05)
    return (gated * scaling[:, None] * norm_gain[None, :]).astype(jnp.bfloat16)


def solution(mesh):
    placed = (P("ctx", "ch"), P("ctx", "ch"), P("ctx", "ch"), P("ctx", "ch"), P("ch"), P("ch"), P())
    return jax.shard_map(
        body, mesh=mesh, in_specs=placed, out_specs=P("ctx", "ch"), check_vma=False
    )
```

```python
import jax
import jax.numpy as jnp
from jax import lax
from jax.experimental import pallas as pl
from jax.experimental.pallas import tpu as pltpu
from jax.sharding import PartitionSpec as P


def placement(pair_list, blocks):
    source = pair_list[:, 0]
    target = pair_list[:, 1]
    runner = pair_list[:, 2]
    slots = lax.iota(jnp.int32, blocks)
    on_diag = source == target
    holds = on_diag[:, None] & (runner[:, None] == slots[None, :])
    holder = jnp.sum(jnp.where(holds, source[:, None], 0), axis=0)
    keeps = on_diag[:, None] & (source[:, None] == slots[None, :])
    device_of = jnp.sum(jnp.where(keeps, runner[:, None], 0), axis=0)
    return holder, device_of


def to_bf16_grid(values):
    return lax.reduce_precision(values, exponent_bits=8, mantissa_bits=7)


def conv_kernel(width, window_ref, signal_ref, out_ref):
    rows = out_ref.shape[0]
    lanes = out_ref.shape[1]
    blocks = window_ref.shape[0]
    signal = signal_ref[...].astype(jnp.float32)
    lane = lax.broadcasted_iota(jnp.int32, (rows, lanes), 1)

    def step(lag, total):
        window = jnp.broadcast_to(window_ref[pl.ds(lag, 1), :], (rows, 2 * rows))
        skewed = pltpu.roll(window, rows + 1, 1, stride=1, stride_axis=0)
        block = skewed[:, :rows]
        block_hi = block.astype(jnp.bfloat16)
        block_lo = (block - block_hi.astype(jnp.float32)).astype(jnp.bfloat16)
        moved = pltpu.roll(signal, lag * width, 1)
        moved = jnp.where(lane >= lag * width, moved, 0.0).astype(jnp.bfloat16)
        pair = jnp.concatenate([block_hi, block_lo], axis=1)
        both = jnp.concatenate([moved, moved], axis=0)
        return total + jnp.dot(pair, both, preferred_element_type=jnp.float32)

    out_ref[...] = lax.fori_loop(
        0, blocks, step, jnp.zeros((rows, lanes), jnp.float32), unroll=2
    )


def causal_conv(window, signal, width):
    rows, lanes = signal.shape
    blocks = window.shape[0]
    return pl.pallas_call(
        lambda *refs: conv_kernel(width, *refs),
        out_shape=jax.ShapeDtypeStruct((rows, lanes), jnp.float32),
        in_specs=[pl.BlockSpec(memory_space=pltpu.VMEM)] * 2,
        out_specs=pl.BlockSpec(memory_space=pltpu.VMEM),
        cost_estimate=pl.CostEstimate(
            flops=4 * rows * rows * lanes * blocks,
            bytes_accessed=window.size * 4 + signal.size * 2 + rows * lanes * 4,
            transcendentals=0,
        ),
    )(window, signal)


def body(query, key, value, filter_taps, conv_bias, norm_gain, pair_list):
    rows = query.shape[0]
    channels = query.shape[1]
    groups = filter_taps.shape[1]
    blocks = lax.axis_size("ctx")
    width = channels // blocks
    share = (channels // groups) // width
    holder, device_of = placement(pair_list, blocks)

    product = to_bf16_grid(key.astype(jnp.float32) * value.astype(jnp.float32))
    signal = product.astype(jnp.bfloat16)

    taps_hi = to_bf16_grid(filter_taps)
    taps_lo = filter_taps - taps_hi
    coded = jnp.stack([taps_hi.T, taps_lo.T], axis=1).reshape(groups, 2, rows // width, width)
    coded = jnp.repeat(coded, share, axis=0).reshape(blocks, 2 * rows // width, width)
    coded = coded.transpose(1, 0, 2).reshape(2 * rows // width, channels)
    outgoing = jnp.concatenate([signal, coded.astype(jnp.bfloat16)], axis=0)

    incoming = lax.all_to_all(outgoing, "ctx", 1, 0, tiled=True)
    incoming = incoming.reshape(blocks, rows + 2 * rows // width, width)
    in_order = incoming[:, :rows, :][device_of]
    taps_in = incoming[:, rows:, :].astype(jnp.float32).reshape(blocks, 2, rows)
    my_taps = taps_in[:, 0, :] + taps_in[:, 1, :]
    earlier = jnp.concatenate([jnp.zeros((1, rows), jnp.float32), my_taps[:-1]], axis=0)
    window = jnp.concatenate([earlier, my_taps], axis=1)[:, ::-1]

    lined = in_order.transpose(1, 0, 2).reshape(rows, blocks * width)
    conv = causal_conv(window, lined, width)
    conv = conv.reshape(rows, blocks, width)[:, holder, :]
    conv = lax.all_to_all(conv, "ctx", 1, 1, tiled=True).reshape(rows, channels)

    long_conv = conv + conv_bias[None, :] * product
    gated = query.astype(jnp.float32) * long_conv
    squares = jnp.sum(gated * gated, axis=1)
    total_sq = jnp.sum(lax.all_gather(squares, "ch"), axis=0)
    scaling = lax.rsqrt(total_sq / (channels * lax.axis_size("ch")) + 1e-05)
    return (gated * scaling[:, None] * norm_gain[None, :]).astype(jnp.bfloat16)


def solution(mesh):
    placed = (P("ctx", "ch"), P("ctx", "ch"), P("ctx", "ch"), P("ctx", "ch"), P("ch"), P("ch"), P())
    return jax.shard_map(
        body, mesh=mesh, in_specs=placed, out_specs=P("ctx", "ch"), check_vma=False
    )
```

```python
import jax
import jax.numpy as jnp
from jax import lax
from jax.experimental import pallas as pl
from jax.experimental.pallas import tpu as pltpu
from jax.sharding import PartitionSpec as P


def placement(pair_list, blocks):
    source = pair_list[:, 0]
    target = pair_list[:, 1]
    runner = pair_list[:, 2]
    slots = lax.iota(jnp.int32, blocks)
    on_diag = source == target
    holds = on_diag[:, None] & (runner[:, None] == slots[None, :])
    holder = jnp.sum(jnp.where(holds, source[:, None], 0), axis=0)
    keeps = on_diag[:, None] & (source[:, None] == slots[None, :])
    device_of = jnp.sum(jnp.where(keeps, runner[:, None], 0), axis=0)
    return holder, device_of


def to_bf16_grid(values):
    return lax.reduce_precision(values, exponent_bits=8, mantissa_bits=7)


def conv_kernel(width, window_ref, signal_ref, out_ref, padded_ref):
    rows = out_ref.shape[1]
    lanes = out_ref.shape[0]
    blocks = window_ref.shape[0]
    padded_ref[pl.ds(0, lanes), :] = jnp.zeros((lanes, rows), jnp.float32)
    padded_ref[pl.ds(lanes, lanes), :] = signal_ref[...].astype(jnp.float32)

    def step(lag, total):
        window = jnp.broadcast_to(window_ref[pl.ds(lag, 1), :], (rows, 2 * rows))
        block = pltpu.roll(window, rows, 1, stride=1, stride_axis=0)[:, :rows]
        block_hi = block.astype(jnp.bfloat16)
        block_lo = (block - block_hi.astype(jnp.float32)).astype(jnp.bfloat16)
        start = pl.multiple_of(lanes - lag * width, width)
        moved = padded_ref[pl.ds(start, lanes), :].astype(jnp.bfloat16)
        total = total + jnp.dot(moved, block_hi, preferred_element_type=jnp.float32)
        return total + jnp.dot(moved, block_lo, preferred_element_type=jnp.float32)

    out_ref[...] = lax.fori_loop(
        0, blocks, step, jnp.zeros((lanes, rows), jnp.float32), unroll=2
    )


def causal_conv(window, signal, width):
    lanes, rows = signal.shape
    blocks = window.shape[0]
    return pl.pallas_call(
        lambda *refs: conv_kernel(width, *refs),
        out_shape=jax.ShapeDtypeStruct((lanes, rows), jnp.float32),
        in_specs=[pl.BlockSpec(memory_space=pltpu.VMEM)] * 2,
        out_specs=pl.BlockSpec(memory_space=pltpu.VMEM),
        scratch_shapes=[pltpu.VMEM((2 * lanes, rows), jnp.float32)],
        cost_estimate=pl.CostEstimate(
            flops=4 * rows * rows * lanes * blocks,
            bytes_accessed=window.size * 4 + signal.size * 2 + rows * lanes * 4,
            transcendentals=0,
        ),
    )(window, signal)


def body(query, key, value, filter_taps, conv_bias, norm_gain, pair_list):
    rows = query.shape[0]
    channels = query.shape[1]
    groups = filter_taps.shape[1]
    blocks = lax.axis_size("ctx")
    width = channels // blocks
    share = (channels // groups) // width
    holder, device_of = placement(pair_list, blocks)

    product = to_bf16_grid(key.astype(jnp.float32) * value.astype(jnp.float32))
    signal = product.astype(jnp.bfloat16)

    taps_hi = to_bf16_grid(filter_taps)
    taps_lo = filter_taps - taps_hi
    coded = jnp.stack([taps_hi.T, taps_lo.T], axis=1).reshape(groups, 2, rows // width, width)
    coded = jnp.repeat(coded, share, axis=0).reshape(blocks, 2 * rows // width, width)
    coded = coded.transpose(1, 0, 2).reshape(2 * rows // width, channels)
    outgoing = jnp.concatenate([signal, coded.astype(jnp.bfloat16)], axis=0)

    incoming = lax.all_to_all(outgoing, "ctx", 1, 0, tiled=True)
    incoming = incoming.reshape(blocks, rows + 2 * rows // width, width)
    in_order = incoming[:, :rows, :][device_of]
    taps_in = incoming[:, rows:, :].astype(jnp.float32).reshape(blocks, 2, rows)
    my_taps = taps_in[:, 0, :] + taps_in[:, 1, :]
    earlier = jnp.concatenate([jnp.zeros((1, rows), jnp.float32), my_taps[:-1]], axis=0)
    window = jnp.concatenate([earlier, my_taps], axis=1)

    lined = in_order.transpose(0, 2, 1).reshape(blocks * width, rows)
    conv = causal_conv(window, lined, width)
    conv = conv.reshape(blocks, width, rows)[holder]
    conv = lax.all_to_all(conv, "ctx", 0, 0, tiled=True)
    conv = conv.transpose(2, 0, 1).reshape(rows, channels)

    long_conv = conv + conv_bias[None, :] * product
    gated = query.astype(jnp.float32) * long_conv
    squares = jnp.sum(gated * gated, axis=1)
    total_sq = jnp.sum(lax.all_gather(squares, "ch"), axis=0)
    scaling = lax.rsqrt(total_sq / (channels * lax.axis_size("ch")) + 1e-05)
    return (gated * scaling[:, None] * norm_gain[None, :]).astype(jnp.bfloat16)


def solution(mesh):
    placed = (P("ctx", "ch"), P("ctx", "ch"), P("ctx", "ch"), P("ctx", "ch"), P("ch"), P("ch"), P())
    return jax.shard_map(
        body, mesh=mesh, in_specs=placed, out_specs=P("ctx", "ch"), check_vma=False
    )
```

```python
import jax
import jax.numpy as jnp
from jax import lax
from jax.experimental import pallas as pl
from jax.experimental.pallas import tpu as pltpu
from jax.sharding import PartitionSpec as P


def placement(pair_list, blocks):
    source = pair_list[:, 0]
    target = pair_list[:, 1]
    runner = pair_list[:, 2]
    slots = lax.iota(jnp.int32, blocks)
    on_diag = source == target
    holds = on_diag[:, None] & (runner[:, None] == slots[None, :])
    holder = jnp.sum(jnp.where(holds, source[:, None], 0), axis=0)
    keeps = on_diag[:, None] & (source[:, None] == slots[None, :])
    device_of = jnp.sum(jnp.where(keeps, runner[:, None], 0), axis=0)
    return holder, device_of


def to_bf16_grid(values):
    return lax.reduce_precision(values, exponent_bits=8, mantissa_bits=7)


def conv_kernel(width, window_ref, signal_ref, out_ref, padded_ref):
    rows = out_ref.shape[1]
    lanes = out_ref.shape[0]
    blocks = window_ref.shape[0]
    padded_ref[pl.ds(0, lanes), :] = jnp.zeros((lanes, rows), jnp.float32)
    padded_ref[pl.ds(lanes, lanes), :] = signal_ref[...].astype(jnp.float32)

    def step(lag, total):
        window = jnp.broadcast_to(window_ref[pl.ds(lag, 1), :], (rows, 2 * rows))
        block = pltpu.roll(window, rows, 1, stride=1, stride_axis=0)[:, :rows]
        block_hi = block.astype(jnp.bfloat16)
        block_lo = (block - block_hi.astype(jnp.float32)).astype(jnp.bfloat16)
        start = pl.multiple_of(lanes - lag * width, width)
        moved = padded_ref[pl.ds(start, lanes), :].astype(jnp.bfloat16)
        total = total + jnp.dot(moved, block_hi, preferred_element_type=jnp.float32)
        return total + jnp.dot(moved, block_lo, preferred_element_type=jnp.float32)

    out_ref[...] = lax.fori_loop(
        0, blocks, step, jnp.zeros((lanes, rows), jnp.float32), unroll=2
    )


def causal_conv(window, signal, width):
    lanes, rows = signal.shape
    blocks = window.shape[0]
    return pl.pallas_call(
        lambda *refs: conv_kernel(width, *refs),
        out_shape=jax.ShapeDtypeStruct((lanes, rows), jnp.float32),
        in_specs=[pl.BlockSpec(memory_space=pltpu.VMEM)] * 2,
        out_specs=pl.BlockSpec(memory_space=pltpu.VMEM),
        scratch_shapes=[pltpu.VMEM((2 * lanes, rows), jnp.float32)],
        cost_estimate=pl.CostEstimate(
            flops=4 * rows * rows * lanes * blocks,
            bytes_accessed=window.size * 4 + signal.size * 2 + rows * lanes * 4,
            transcendentals=0,
        ),
    )(window, signal)


def body(query, key, value, filter_taps, conv_bias, norm_gain, pair_list):
    rows = query.shape[0]
    channels = query.shape[1]
    groups = filter_taps.shape[1]
    blocks = lax.axis_size("ctx")
    width = channels // blocks
    share = (channels // groups) // width
    holder, device_of = placement(pair_list, blocks)

    product = to_bf16_grid(key.astype(jnp.float32) * value.astype(jnp.float32))
    signal = product.astype(jnp.bfloat16)

    taps_hi = to_bf16_grid(filter_taps)
    taps_lo = filter_taps - taps_hi
    coded = jnp.stack([taps_hi.T, taps_lo.T], axis=1).reshape(groups, 2, rows // width, width)
    coded = jnp.repeat(coded, share, axis=0).reshape(blocks, 2 * rows // width, width)
    coded = coded.transpose(1, 0, 2).reshape(2 * rows // width, channels)
    outgoing = jnp.concatenate([signal, coded.astype(jnp.bfloat16)], axis=0)

    incoming = lax.all_to_all(outgoing, "ctx", 1, 0, tiled=True)
    incoming = incoming.reshape(blocks, rows + 2 * rows // width, width)
    in_order = incoming[:, :rows, :][device_of]
    taps_in = incoming[:, rows:, :].astype(jnp.float32).reshape(blocks, 2, rows)
    span = 2 * rows
    wide = blocks // 2
    my_taps = (taps_in[:, 0, :] + taps_in[:, 1, :]).reshape(wide, span)
    earlier = jnp.concatenate([jnp.zeros((1, span), jnp.float32), my_taps[:-1]], axis=0)
    window = jnp.concatenate([earlier, my_taps], axis=1)

    lined = in_order.reshape(wide, span, width).transpose(0, 2, 1).reshape(wide * width, span)
    conv = causal_conv(window, lined, width)
    conv = conv.reshape(wide, width, 2, rows).transpose(0, 2, 1, 3).reshape(blocks, width, rows)[holder]
    conv = lax.all_to_all(conv, "ctx", 0, 0, tiled=True)
    conv = conv.transpose(2, 0, 1).reshape(rows, channels)

    long_conv = conv + conv_bias[None, :] * product
    gated = query.astype(jnp.float32) * long_conv
    squares = jnp.sum(gated * gated, axis=1)
    total_sq = jnp.sum(lax.all_gather(squares, "ch"), axis=0)
    scaling = lax.rsqrt(total_sq / (channels * lax.axis_size("ch")) + 1e-05)
    return (gated * scaling[:, None] * norm_gain[None, :]).astype(jnp.bfloat16)


def solution(mesh):
    placed = (P("ctx", "ch"), P("ctx", "ch"), P("ctx", "ch"), P("ctx", "ch"), P("ch"), P("ch"), P())
    return jax.shard_map(
        body, mesh=mesh, in_specs=placed, out_specs=P("ctx", "ch"), check_vma=False
    )
```

```python
import jax
import jax.numpy as jnp
from jax import lax
from jax.experimental import pallas as pl
from jax.experimental.pallas import tpu as pltpu
from jax.sharding import PartitionSpec as P


def placement(pair_list, blocks):
    source = pair_list[:, 0]
    target = pair_list[:, 1]
    runner = pair_list[:, 2]
    slots = lax.iota(jnp.int32, blocks)
    on_diag = source == target
    holds = on_diag[:, None] & (runner[:, None] == slots[None, :])
    holder = jnp.sum(jnp.where(holds, source[:, None], 0), axis=0)
    keeps = on_diag[:, None] & (source[:, None] == slots[None, :])
    device_of = jnp.sum(jnp.where(keeps, runner[:, None], 0), axis=0)
    return holder, device_of


def to_bf16_grid(values):
    return lax.reduce_precision(values, exponent_bits=8, mantissa_bits=7)


def conv_kernel(width, window_ref, signal_ref, out_ref, padded_ref):
    rows = out_ref.shape[1]
    lanes = out_ref.shape[0]
    blocks = window_ref.shape[0]
    padded_ref[pl.ds(0, lanes), :] = jnp.zeros((lanes, rows), jnp.float32)
    padded_ref[pl.ds(lanes, lanes), :] = signal_ref[...].astype(jnp.float32)

    half = lanes // 2

    def lag_block(lag):
        window = jnp.broadcast_to(window_ref[pl.ds(lag, 1), :], (rows, 2 * rows))
        block = pltpu.roll(window, rows, 1, stride=1, stride_axis=0)[:, :rows]
        block_hi = block.astype(jnp.bfloat16)
        block_lo = (block - block_hi.astype(jnp.float32)).astype(jnp.bfloat16)
        return block_hi, block_lo

    def add_lag(total, lag, offset, count):
        block_hi, block_lo = lag_block(lag)
        start = pl.multiple_of(lanes - lag * width + offset, width)
        moved = padded_ref[pl.ds(start, count), :].astype(jnp.bfloat16)
        total = total + jnp.dot(moved, block_hi, preferred_element_type=jnp.float32)
        return total + jnp.dot(moved, block_lo, preferred_element_type=jnp.float32)

    total = lax.fori_loop(
        0, blocks // 2, lambda lag, acc: add_lag(acc, lag, 0, lanes),
        jnp.zeros((lanes, rows), jnp.float32), unroll=2,
    )
    out_ref[pl.ds(0, half), :] = total[:half]
    out_ref[pl.ds(half, half), :] = lax.fori_loop(
        blocks // 2, blocks, lambda lag, acc: add_lag(acc, lag, half, half),
        total[half:], unroll=2,
    )


def causal_conv(window, signal, width):
    lanes, rows = signal.shape
    blocks = window.shape[0]
    return pl.pallas_call(
        lambda *refs: conv_kernel(width, *refs),
        out_shape=jax.ShapeDtypeStruct((lanes, rows), jnp.float32),
        in_specs=[pl.BlockSpec(memory_space=pltpu.VMEM)] * 2,
        out_specs=pl.BlockSpec(memory_space=pltpu.VMEM),
        scratch_shapes=[pltpu.VMEM((2 * lanes, rows), jnp.float32)],
        cost_estimate=pl.CostEstimate(
            flops=4 * rows * rows * lanes * blocks,
            bytes_accessed=window.size * 4 + signal.size * 2 + rows * lanes * 4,
            transcendentals=0,
        ),
    )(window, signal)


def body(query, key, value, filter_taps, conv_bias, norm_gain, pair_list):
    rows = query.shape[0]
    channels = query.shape[1]
    groups = filter_taps.shape[1]
    blocks = lax.axis_size("ctx")
    width = channels // blocks
    share = (channels // groups) // width
    holder, device_of = placement(pair_list, blocks)

    product = to_bf16_grid(key.astype(jnp.float32) * value.astype(jnp.float32))
    signal = product.astype(jnp.bfloat16)

    taps_hi = to_bf16_grid(filter_taps)
    taps_lo = filter_taps - taps_hi
    coded = jnp.stack([taps_hi.T, taps_lo.T], axis=1).reshape(groups, 2, rows // width, width)
    coded = jnp.repeat(coded, share, axis=0).reshape(blocks, 2 * rows // width, width)
    coded = coded.transpose(1, 0, 2).reshape(2 * rows // width, channels)
    outgoing = jnp.concatenate([signal, coded.astype(jnp.bfloat16)], axis=0)

    incoming = lax.all_to_all(outgoing, "ctx", 1, 0, tiled=True)
    incoming = incoming.reshape(blocks, rows + 2 * rows // width, width)
    in_order = incoming[:, :rows, :][device_of]
    taps_in = incoming[:, rows:, :].astype(jnp.float32).reshape(blocks, 2, rows)
    span = 2 * rows
    wide = blocks // 2
    my_taps = (taps_in[:, 0, :] + taps_in[:, 1, :]).reshape(wide, span)
    earlier = jnp.concatenate([jnp.zeros((1, span), jnp.float32), my_taps[:-1]], axis=0)
    window = jnp.concatenate([earlier, my_taps], axis=1)

    lined = in_order.reshape(wide, span, width).transpose(0, 2, 1).reshape(wide * width, span)
    conv = causal_conv(window, lined, width)
    conv = conv.reshape(wide, width, 2, rows).transpose(0, 2, 1, 3).reshape(blocks, width, rows)[holder]
    conv = lax.all_to_all(conv, "ctx", 0, 0, tiled=True)
    conv = conv.transpose(2, 0, 1).reshape(rows, channels)

    long_conv = conv + conv_bias[None, :] * product
    gated = query.astype(jnp.float32) * long_conv
    squares = jnp.sum(gated * gated, axis=1)
    total_sq = jnp.sum(lax.all_gather(squares, "ch"), axis=0)
    scaling = lax.rsqrt(total_sq / (channels * lax.axis_size("ch")) + 1e-05)
    return (gated * scaling[:, None] * norm_gain[None, :]).astype(jnp.bfloat16)


def solution(mesh):
    placed = (P("ctx", "ch"), P("ctx", "ch"), P("ctx", "ch"), P("ctx", "ch"), P("ch"), P("ch"), P())
    return jax.shard_map(
        body, mesh=mesh, in_specs=placed, out_specs=P("ctx", "ch"), check_vma=False
    )
```

```python
import jax
import jax.numpy as jnp
from jax import lax
from jax.experimental import pallas as pl
from jax.experimental.pallas import tpu as pltpu
from jax.sharding import PartitionSpec as P


def placement(pair_list, blocks):
    source = pair_list[:, 0]
    target = pair_list[:, 1]
    runner = pair_list[:, 2]
    slots = lax.iota(jnp.int32, blocks)
    on_diag = source == target
    holds = on_diag[:, None] & (runner[:, None] == slots[None, :])
    holder = jnp.sum(jnp.where(holds, source[:, None], 0), axis=0)
    keeps = on_diag[:, None] & (source[:, None] == slots[None, :])
    device_of = jnp.sum(jnp.where(keeps, runner[:, None], 0), axis=0)
    return holder, device_of


def to_bf16_grid(values):
    return lax.reduce_precision(values, exponent_bits=8, mantissa_bits=7)


def conv_kernel(width, window_ref, signal_ref, out_ref, padded_ref):
    rows = out_ref.shape[1]
    lanes = out_ref.shape[0]
    pairs = window_ref.shape[0]
    half = lanes // 2
    padded_ref[pl.ds(0, lanes), :] = jnp.zeros((lanes, rows), jnp.float32)
    padded_ref[pl.ds(lanes, lanes), :] = signal_ref[...].astype(jnp.float32)

    def add_lag(total, block, lag, offset, count):
        block_hi = block.astype(jnp.bfloat16)
        block_lo = (block - block_hi.astype(jnp.float32)).astype(jnp.bfloat16)
        start = pl.multiple_of(lanes - lag * width + offset, width)
        moved = padded_ref[pl.ds(start, count), :].astype(jnp.bfloat16)
        total = total + jnp.dot(moved, block_hi, preferred_element_type=jnp.float32)
        return total + jnp.dot(moved, block_lo, preferred_element_type=jnp.float32)

    def add_pair(total, pair, offset, count):
        window = jnp.broadcast_to(window_ref[pl.ds(pair, 1), :], (rows, 3 * rows))
        skewed = pltpu.roll(window, 2 * rows, 1, stride=1, stride_axis=0)
        total = add_lag(total, skewed[:, :rows], 2 * pair, offset, count)
        return add_lag(total, skewed[:, rows : 2 * rows], 2 * pair + 1, offset, count)

    total = lax.fori_loop(
        0, pairs // 2, lambda pair, acc: add_pair(acc, pair, 0, lanes),
        jnp.zeros((lanes, rows), jnp.float32),
    )
    out_ref[pl.ds(0, half), :] = total[:half]
    out_ref[pl.ds(half, half), :] = lax.fori_loop(
        pairs // 2, pairs, lambda pair, acc: add_pair(acc, pair, half, half), total[half:],
    )


def causal_conv(window, signal, width):
    lanes, rows = signal.shape
    blocks = 2 * window.shape[0]
    return pl.pallas_call(
        lambda *refs: conv_kernel(width, *refs),
        out_shape=jax.ShapeDtypeStruct((lanes, rows), jnp.float32),
        in_specs=[pl.BlockSpec(memory_space=pltpu.VMEM)] * 2,
        out_specs=pl.BlockSpec(memory_space=pltpu.VMEM),
        scratch_shapes=[pltpu.VMEM((2 * lanes, rows), jnp.float32)],
        cost_estimate=pl.CostEstimate(
            flops=4 * rows * rows * lanes * blocks,
            bytes_accessed=window.size * 4 + signal.size * 2 + rows * lanes * 4,
            transcendentals=0,
        ),
    )(window, signal)


def body(query, key, value, filter_taps, conv_bias, norm_gain, pair_list):
    rows = query.shape[0]
    channels = query.shape[1]
    groups = filter_taps.shape[1]
    blocks = lax.axis_size("ctx")
    width = channels // blocks
    share = (channels // groups) // width
    holder, device_of = placement(pair_list, blocks)

    product = to_bf16_grid(key.astype(jnp.float32) * value.astype(jnp.float32))
    signal = product.astype(jnp.bfloat16)

    taps_hi = to_bf16_grid(filter_taps)
    taps_lo = filter_taps - taps_hi
    coded = jnp.stack([taps_hi.T, taps_lo.T], axis=1).reshape(groups, 2, rows // width, width)
    coded = jnp.repeat(coded, share, axis=0).reshape(blocks, 2 * rows // width, width)
    coded = coded.transpose(1, 0, 2).reshape(2 * rows // width, channels)
    outgoing = jnp.concatenate([signal, coded.astype(jnp.bfloat16)], axis=0)

    incoming = lax.all_to_all(outgoing, "ctx", 1, 0, tiled=True)
    incoming = incoming.reshape(blocks, rows + 2 * rows // width, width)
    in_order = incoming[:, :rows, :][device_of]
    taps_in = incoming[:, rows:, :].astype(jnp.float32).reshape(blocks, 2, rows)
    span = 2 * rows
    wide = blocks // 2
    my_taps = (taps_in[:, 0, :] + taps_in[:, 1, :]).reshape(wide, span)
    shifted = jnp.concatenate([jnp.zeros((1, span), jnp.float32), my_taps], axis=0)
    window = jnp.concatenate([shifted[0:-1:2], shifted[1::2], shifted[2::2]], axis=1)

    lined = in_order.reshape(wide, span, width).transpose(0, 2, 1).reshape(wide * width, span)
    conv = causal_conv(window, lined, width)
    conv = conv.reshape(wide, width, 2, rows).transpose(0, 2, 1, 3).reshape(blocks, width, rows)[holder]
    conv = lax.all_to_all(conv, "ctx", 0, 0, tiled=True)
    conv = conv.transpose(2, 0, 1).reshape(rows, channels)

    long_conv = conv + conv_bias[None, :] * product
    gated = query.astype(jnp.float32) * long_conv
    squares = jnp.sum(gated * gated, axis=1)
    total_sq = jnp.sum(lax.all_gather(squares, "ch"), axis=0)
    scaling = lax.rsqrt(total_sq / (channels * lax.axis_size("ch")) + 1e-05)
    return (gated * scaling[:, None] * norm_gain[None, :]).astype(jnp.bfloat16)


def solution(mesh):
    placed = (P("ctx", "ch"), P("ctx", "ch"), P("ctx", "ch"), P("ctx", "ch"), P("ch"), P("ch"), P())
    return jax.shard_map(
        body, mesh=mesh, in_specs=placed, out_specs=P("ctx", "ch"), check_vma=False
    )
```

```python
import jax
import jax.numpy as jnp
from jax import lax
from jax.experimental import pallas as pl
from jax.experimental.pallas import tpu as pltpu
from jax.sharding import PartitionSpec as P


def placement(pair_list, blocks):
    source = pair_list[:, 0]
    target = pair_list[:, 1]
    runner = pair_list[:, 2]
    slots = lax.iota(jnp.int32, blocks)
    on_diag = source == target
    holds = on_diag[:, None] & (runner[:, None] == slots[None, :])
    holder = jnp.sum(jnp.where(holds, source[:, None], 0), axis=0)
    keeps = on_diag[:, None] & (source[:, None] == slots[None, :])
    device_of = jnp.sum(jnp.where(keeps, runner[:, None], 0), axis=0)
    return holder, device_of


def to_bf16_grid(values):
    return lax.reduce_precision(values, exponent_bits=8, mantissa_bits=7)


def conv_kernel(width, device_ref, window_ref, signal_ref, out_ref, padded_ref):
    rows = signal_ref.shape[1]
    lanes = signal_ref.shape[0]
    pairs = window_ref.shape[0]
    part = out_ref.shape[2]
    half = lanes // 2
    padded_ref[pl.ds(0, lanes), :] = jnp.zeros((lanes, rows), jnp.float32)
    padded_ref[pl.ds(lanes, lanes), :] = signal_ref[...].astype(jnp.float32)

    def add_lag(total, block, lag, offset, count):
        block_hi = block.astype(jnp.bfloat16)
        block_lo = (block - block_hi.astype(jnp.float32)).astype(jnp.bfloat16)
        start = pl.multiple_of(lanes - lag * width + offset, width)
        moved = padded_ref[pl.ds(start, count), :].astype(jnp.bfloat16)
        total = total + jnp.dot(moved, block_hi, preferred_element_type=jnp.float32)
        return total + jnp.dot(moved, block_lo, preferred_element_type=jnp.float32)

    def add_pair(total, pair, offset, count):
        window = jnp.broadcast_to(window_ref[pl.ds(pair, 1), :], (rows, 3 * rows))
        skewed = pltpu.roll(window, 2 * rows, 1, stride=1, stride_axis=0)
        total = add_lag(total, skewed[:, :rows], 2 * pair, offset, count)
        return add_lag(total, skewed[:, rows : 2 * rows], 2 * pair + 1, offset, count)

    total = lax.fori_loop(
        0, pairs // 2, lambda pair, acc: add_pair(acc, pair, 0, lanes),
        jnp.zeros((lanes, rows), jnp.float32),
    )
    lower = lax.fori_loop(
        pairs // 2, pairs, lambda pair, acc: add_pair(acc, pair, half, half), total[half:],
    )

    def place(values, first):
        for row in range(values.shape[0] // width):
            for piece in range(rows // part):
                block = (first + row) * (rows // part) + piece
                out_ref[device_ref[block]] = values[
                    row * width : (row + 1) * width, piece * part : (piece + 1) * part
                ]

    place(total[:half], 0)
    place(lower, half // width)


def causal_conv(device_of, window, signal, width, part):
    lanes, rows = signal.shape
    blocks = 2 * window.shape[0]
    return pl.pallas_call(
        lambda *refs: conv_kernel(width, *refs),
        out_shape=jax.ShapeDtypeStruct((lanes * rows // (width * part), width, part), jnp.float32),
        in_specs=[pl.BlockSpec(memory_space=pltpu.SMEM)] + [pl.BlockSpec(memory_space=pltpu.VMEM)] * 2,
        out_specs=pl.BlockSpec(memory_space=pltpu.VMEM),
        scratch_shapes=[pltpu.VMEM((2 * lanes, rows), jnp.float32)],
        cost_estimate=pl.CostEstimate(
            flops=4 * rows * rows * lanes * blocks,
            bytes_accessed=window.size * 4 + signal.size * 2 + rows * lanes * 4,
            transcendentals=0,
        ),
    )(device_of, window, signal)


def body(query, key, value, filter_taps, conv_bias, norm_gain, pair_list):
    rows = query.shape[0]
    channels = query.shape[1]
    groups = filter_taps.shape[1]
    blocks = lax.axis_size("ctx")
    width = channels // blocks
    share = (channels // groups) // width
    holder, device_of = placement(pair_list, blocks)

    product = to_bf16_grid(key.astype(jnp.float32) * value.astype(jnp.float32))
    signal = product.astype(jnp.bfloat16)

    taps_hi = to_bf16_grid(filter_taps)
    taps_lo = filter_taps - taps_hi
    coded = jnp.stack([taps_hi.T, taps_lo.T], axis=1).reshape(groups, 2, rows // width, width)
    coded = jnp.repeat(coded, share, axis=0).reshape(blocks, 2 * rows // width, width)
    coded = coded.transpose(1, 0, 2).reshape(2 * rows // width, channels)
    outgoing = jnp.concatenate([signal, coded.astype(jnp.bfloat16)], axis=0)

    incoming = lax.all_to_all(outgoing, "ctx", 1, 0, tiled=True)
    incoming = incoming.reshape(blocks, rows + 2 * rows // width, width)
    in_order = incoming[:, :rows, :][device_of]
    taps_in = incoming[:, rows:, :].astype(jnp.float32).reshape(blocks, 2, rows)
    span = 2 * rows
    wide = blocks // 2
    my_taps = (taps_in[:, 0, :] + taps_in[:, 1, :]).reshape(wide, span)
    shifted = jnp.concatenate([jnp.zeros((1, span), jnp.float32), my_taps], axis=0)
    window = jnp.concatenate([shifted[0:-1:2], shifted[1::2], shifted[2::2]], axis=1)

    lined = in_order.reshape(wide, span, width).transpose(0, 2, 1).reshape(wide * width, span)
    conv = causal_conv(device_of, window, lined, width, rows)
    conv = lax.all_to_all(conv, "ctx", 0, 0, tiled=True)
    conv = conv.transpose(2, 0, 1).reshape(rows, channels)

    long_conv = conv + conv_bias[None, :] * product
    gated = query.astype(jnp.float32) * long_conv
    squares = jnp.sum(gated * gated, axis=1)
    total_sq = jnp.sum(lax.all_gather(squares, "ch"), axis=0)
    scaling = lax.rsqrt(total_sq / (channels * lax.axis_size("ch")) + 1e-05)
    return (gated * scaling[:, None] * norm_gain[None, :]).astype(jnp.bfloat16)


def solution(mesh):
    placed = (P("ctx", "ch"), P("ctx", "ch"), P("ctx", "ch"), P("ctx", "ch"), P("ch"), P("ch"), P())
    return jax.shard_map(
        body, mesh=mesh, in_specs=placed, out_specs=P("ctx", "ch"), check_vma=False
    )
```

```python
import jax
import jax.numpy as jnp
from jax import lax
from jax.experimental import pallas as pl
from jax.experimental.pallas import tpu as pltpu
from jax.sharding import PartitionSpec as P


def placement(pair_list, blocks):
    source = pair_list[:, 0]
    target = pair_list[:, 1]
    runner = pair_list[:, 2]
    slots = lax.iota(jnp.int32, blocks)
    on_diag = source == target
    holds = on_diag[:, None] & (runner[:, None] == slots[None, :])
    holder = jnp.sum(jnp.where(holds, source[:, None], 0), axis=0)
    keeps = on_diag[:, None] & (source[:, None] == slots[None, :])
    device_of = jnp.sum(jnp.where(keeps, runner[:, None], 0), axis=0)
    return holder, device_of


def to_bf16_grid(values):
    return lax.reduce_precision(values, exponent_bits=8, mantissa_bits=7)


def conv_kernel(width, device_ref, window_ref, incoming_ref, out_ref, padded_ref):
    rows = window_ref.shape[1] // 3
    pairs = window_ref.shape[0]
    part = out_ref.shape[2]
    lanes = 2 * pairs * width
    half = lanes // 2
    padded_ref[pl.ds(0, lanes), :] = jnp.zeros((lanes, rows), jnp.float32)
    for block in range(incoming_ref.shape[0]):
        line = lanes + (block // (rows // part)) * width
        column = (block % (rows // part)) * part
        padded_ref[pl.ds(line, width), pl.ds(column, part)] = incoming_ref[
            device_ref[block], pl.ds(0, width), :
        ].astype(jnp.float32)

    def add_lag(total, block, lag, offset, count):
        block_hi = block.astype(jnp.bfloat16)
        block_lo = (block - block_hi.astype(jnp.float32)).astype(jnp.bfloat16)
        start = pl.multiple_of(lanes - lag * width + offset, width)
        moved = padded_ref[pl.ds(start, count), :].astype(jnp.bfloat16)
        total = total + jnp.dot(moved, block_hi, preferred_element_type=jnp.float32)
        return total + jnp.dot(moved, block_lo, preferred_element_type=jnp.float32)

    def add_pair(total, pair, offset, count):
        window = jnp.broadcast_to(window_ref[pl.ds(pair, 1), :], (rows, 3 * rows))
        skewed = pltpu.roll(window, 2 * rows, 1, stride=1, stride_axis=0)
        total = add_lag(total, skewed[:, :rows], 2 * pair, offset, count)
        return add_lag(total, skewed[:, rows : 2 * rows], 2 * pair + 1, offset, count)

    total = lax.fori_loop(
        0, pairs // 2, lambda pair, acc: add_pair(acc, pair, 0, lanes),
        jnp.zeros((lanes, rows), jnp.float32),
    )
    lower = lax.fori_loop(
        pairs // 2, pairs, lambda pair, acc: add_pair(acc, pair, half, half), total[half:],
    )

    def place(values, first):
        for row in range(values.shape[0] // width):
            for piece in range(rows // part):
                block = (first + row) * (rows // part) + piece
                out_ref[device_ref[block]] = values[
                    row * width : (row + 1) * width, piece * part : (piece + 1) * part
                ]

    place(total[:half], 0)
    place(lower, half // width)


def causal_conv(device_of, window, incoming, width):
    blocks, _, part = incoming.shape
    rows = window.shape[1] // 3
    lanes = blocks * part // rows * width
    return pl.pallas_call(
        lambda *refs: conv_kernel(width, *refs),
        out_shape=jax.ShapeDtypeStruct((blocks, width, part), jnp.float32),
        in_specs=[pl.BlockSpec(memory_space=pltpu.SMEM)] + [pl.BlockSpec(memory_space=pltpu.VMEM)] * 2,
        out_specs=pl.BlockSpec(memory_space=pltpu.VMEM),
        scratch_shapes=[pltpu.VMEM((2 * lanes, rows), jnp.float32)],
        cost_estimate=pl.CostEstimate(
            flops=4 * rows * rows * lanes * 2 * window.shape[0],
            bytes_accessed=window.size * 4 + incoming.size * 2 + rows * lanes * 4,
            transcendentals=0,
        ),
    )(device_of, window, incoming)


def body(query, key, value, filter_taps, conv_bias, norm_gain, pair_list):
    rows = query.shape[0]
    channels = query.shape[1]
    groups = filter_taps.shape[1]
    blocks = lax.axis_size("ctx")
    width = channels // blocks
    share = (channels // groups) // width
    holder, device_of = placement(pair_list, blocks)

    product = to_bf16_grid(key.astype(jnp.float32) * value.astype(jnp.float32))
    signal = product.astype(jnp.bfloat16)

    taps_hi = to_bf16_grid(filter_taps)
    taps_lo = filter_taps - taps_hi
    coded = jnp.repeat(jnp.stack([taps_hi.T, taps_lo.T], axis=1), share, axis=0)
    tile = 16
    outgoing = jnp.concatenate(
        [
            signal.T.reshape(blocks, width, rows),
            coded.astype(jnp.bfloat16),
            jnp.zeros((blocks, tile - width - 2, rows), jnp.bfloat16),
        ],
        axis=1,
    )
    incoming = lax.all_to_all(outgoing, "ctx", 0, 0, tiled=True)
    taps_in = incoming[:, width : width + 2, :].astype(jnp.float32)
    span = 2 * rows
    wide = blocks // 2
    my_taps = (taps_in[:, 0, :] + taps_in[:, 1, :]).reshape(wide, span)
    shifted = jnp.concatenate([jnp.zeros((1, span), jnp.float32), my_taps], axis=0)
    window = jnp.concatenate([shifted[0:-1:2], shifted[1::2], shifted[2::2]], axis=1)

    conv = causal_conv(device_of, window, incoming, width)
    conv = lax.all_to_all(conv, "ctx", 0, 0, tiled=True)
    conv = conv.transpose(2, 0, 1).reshape(rows, channels)

    long_conv = conv + conv_bias[None, :] * product
    gated = query.astype(jnp.float32) * long_conv
    squares = jnp.sum(gated * gated, axis=1)
    total_sq = jnp.sum(lax.all_gather(squares, "ch"), axis=0)
    scaling = lax.rsqrt(total_sq / (channels * lax.axis_size("ch")) + 1e-05)
    return (gated * scaling[:, None] * norm_gain[None, :]).astype(jnp.bfloat16)


def solution(mesh):
    placed = (P("ctx", "ch"), P("ctx", "ch"), P("ctx", "ch"), P("ctx", "ch"), P("ch"), P("ch"), P())
    return jax.shard_map(
        body, mesh=mesh, in_specs=placed, out_specs=P("ctx", "ch"), check_vma=False
    )
```

```python
import jax
import jax.numpy as jnp
from jax import lax
from jax.experimental import pallas as pl
from jax.experimental.pallas import tpu as pltpu
from jax.sharding import PartitionSpec as P


def placement(pair_list, blocks):
    source = pair_list[:, 0]
    target = pair_list[:, 1]
    runner = pair_list[:, 2]
    slots = lax.iota(jnp.int32, blocks)
    on_diag = source == target
    holds = on_diag[:, None] & (runner[:, None] == slots[None, :])
    holder = jnp.sum(jnp.where(holds, source[:, None], 0), axis=0)
    keeps = on_diag[:, None] & (source[:, None] == slots[None, :])
    device_of = jnp.sum(jnp.where(keeps, runner[:, None], 0), axis=0)
    return holder, device_of


def to_bf16_grid(values):
    return lax.reduce_precision(values, exponent_bits=8, mantissa_bits=7)


def conv_kernel(width, device_ref, window_ref, window_lo_ref, incoming_ref, out_ref, padded_ref):
    rows = window_ref.shape[1] // 3
    pairs = window_ref.shape[0]
    part = out_ref.shape[2]
    lanes = 2 * pairs * width
    half = lanes // 2
    padded_ref[pl.ds(0, lanes), :] = jnp.zeros((lanes, rows), jnp.float32)
    for block in range(incoming_ref.shape[0]):
        line = lanes + (block // (rows // part)) * width
        column = (block % (rows // part)) * part
        padded_ref[pl.ds(line, width), pl.ds(column, part)] = incoming_ref[
            device_ref[block], pl.ds(0, width), :
        ].astype(jnp.float32)

    def add_lag(total, block_hi, block_lo, lag, offset, count):
        start = pl.multiple_of(lanes - lag * width + offset, width)
        moved = padded_ref[pl.ds(start, count), :].astype(jnp.bfloat16)
        total = total + jnp.dot(moved, block_hi, preferred_element_type=jnp.float32)
        return total + jnp.dot(moved, block_lo, preferred_element_type=jnp.float32)

    def skew(ref, pair):
        window = jnp.broadcast_to(ref[pl.ds(pair, 1), :], (rows, 3 * rows))
        return pltpu.roll(window, 2 * rows, 1, stride=1, stride_axis=0)

    def add_pair(total, pair, offset, count):
        high = skew(window_ref, pair)
        low = skew(window_lo_ref, pair)
        first = (high[:, :rows].astype(jnp.bfloat16), low[:, :rows].astype(jnp.bfloat16))
        total = add_lag(total, *first, 2 * pair, offset, count)
        second = (
            high[:, rows : 2 * rows].astype(jnp.bfloat16),
            low[:, rows : 2 * rows].astype(jnp.bfloat16),
        )
        return add_lag(total, *second, 2 * pair + 1, offset, count)

    total = lax.fori_loop(
        0, pairs // 2, lambda pair, acc: add_pair(acc, pair, 0, lanes),
        jnp.zeros((lanes, rows), jnp.float32),
    )
    lower = lax.fori_loop(
        pairs // 2, pairs, lambda pair, acc: add_pair(acc, pair, half, half), total[half:],
    )

    def place(values, first):
        for row in range(values.shape[0] // width):
            for piece in range(rows // part):
                block = (first + row) * (rows // part) + piece
                out_ref[device_ref[block]] = values[
                    row * width : (row + 1) * width, piece * part : (piece + 1) * part
                ]

    place(total[:half], 0)
    place(lower, half // width)


def causal_conv(device_of, window, incoming, width):
    window_hi = to_bf16_grid(window)
    window_lo = to_bf16_grid(window - window_hi)
    blocks, _, part = incoming.shape
    rows = window.shape[1] // 3
    lanes = blocks * part // rows * width
    return pl.pallas_call(
        lambda *refs: conv_kernel(width, *refs),
        out_shape=jax.ShapeDtypeStruct((blocks, width, part), jnp.float32),
        in_specs=[pl.BlockSpec(memory_space=pltpu.SMEM)] + [pl.BlockSpec(memory_space=pltpu.VMEM)] * 3,
        out_specs=pl.BlockSpec(memory_space=pltpu.VMEM),
        scratch_shapes=[pltpu.VMEM((2 * lanes, rows), jnp.float32)],
        cost_estimate=pl.CostEstimate(
            flops=4 * rows * rows * lanes * 2 * window.shape[0],
            bytes_accessed=window.size * 4 + incoming.size * 2 + rows * lanes * 4,
            transcendentals=0,
        ),
    )(device_of, window_hi, window_lo, incoming)


def body(query, key, value, filter_taps, conv_bias, norm_gain, pair_list):
    rows = query.shape[0]
    channels = query.shape[1]
    groups = filter_taps.shape[1]
    blocks = lax.axis_size("ctx")
    width = channels // blocks
    share = (channels // groups) // width
    holder, device_of = placement(pair_list, blocks)

    product = to_bf16_grid(key.astype(jnp.float32) * value.astype(jnp.float32))
    signal = product.astype(jnp.bfloat16)

    taps_hi = to_bf16_grid(filter_taps)
    taps_lo = filter_taps - taps_hi
    coded = jnp.repeat(jnp.stack([taps_hi.T, taps_lo.T], axis=1), share, axis=0)
    tile = 16
    outgoing = jnp.concatenate(
        [
            signal.T.reshape(blocks, width, rows),
            coded.astype(jnp.bfloat16),
            jnp.zeros((blocks, tile - width - 2, rows), jnp.bfloat16),
        ],
        axis=1,
    )
    incoming = lax.all_to_all(outgoing, "ctx", 0, 0, tiled=True)
    taps_in = incoming[:, width : width + 2, :].astype(jnp.float32)
    span = 2 * rows
    wide = blocks // 2
    my_taps = (taps_in[:, 0, :] + taps_in[:, 1, :]).reshape(wide, span)
    shifted = jnp.concatenate([jnp.zeros((1, span), jnp.float32), my_taps], axis=0)
    window = jnp.concatenate([shifted[0:-1:2], shifted[1::2], shifted[2::2]], axis=1)

    conv = causal_conv(device_of, window, incoming, width)
    conv = lax.all_to_all(conv, "ctx", 0, 0, tiled=True)
    conv = conv.transpose(2, 0, 1).reshape(rows, channels)

    long_conv = conv + conv_bias[None, :] * product
    gated = query.astype(jnp.float32) * long_conv
    squares = jnp.sum(gated * gated, axis=1)
    total_sq = jnp.sum(lax.all_gather(squares, "ch"), axis=0)
    scaling = lax.rsqrt(total_sq / (channels * lax.axis_size("ch")) + 1e-05)
    return (gated * scaling[:, None] * norm_gain[None, :]).astype(jnp.bfloat16)


def solution(mesh):
    placed = (P("ctx", "ch"), P("ctx", "ch"), P("ctx", "ch"), P("ctx", "ch"), P("ch"), P("ch"), P())
    return jax.shard_map(
        body, mesh=mesh, in_specs=placed, out_specs=P("ctx", "ch"), check_vma=False
    )
```

```python
import jax
import jax.numpy as jnp
from jax import lax
from jax.experimental import pallas as pl
from jax.experimental.pallas import tpu as pltpu
from jax.sharding import PartitionSpec as P


def placement(pair_list, blocks):
    source = pair_list[:, 0]
    target = pair_list[:, 1]
    runner = pair_list[:, 2]
    slots = lax.iota(jnp.int32, blocks)
    on_diag = source == target
    holds = on_diag[:, None] & (runner[:, None] == slots[None, :])
    holder = jnp.sum(jnp.where(holds, source[:, None], 0), axis=0)
    keeps = on_diag[:, None] & (source[:, None] == slots[None, :])
    device_of = jnp.sum(jnp.where(keeps, runner[:, None], 0), axis=0)
    return holder, device_of


def to_bf16_grid(values):
    return lax.reduce_precision(values, exponent_bits=8, mantissa_bits=7)


def conv_kernel(width, device_ref, window_ref, window_lo_ref, incoming_ref, out_ref, padded_ref):
    rows = window_ref.shape[1] // 3
    pairs = window_ref.shape[0]
    part = out_ref.shape[2]
    lanes = 2 * pairs * width
    half = lanes // 2
    padded_ref[pl.ds(0, lanes), :] = jnp.zeros((lanes, rows), jnp.float32)
    for block in range(incoming_ref.shape[0]):
        line = lanes + (block // (rows // part)) * width
        column = (block % (rows // part)) * part
        padded_ref[pl.ds(line, width), pl.ds(column, part)] = incoming_ref[
            device_ref[block], pl.ds(0, width), :
        ].astype(jnp.float32)

    def add_lag(total, block_hi, block_lo, lag, offset, count):
        start = pl.multiple_of(lanes - lag * width + offset, width)
        moved = padded_ref[pl.ds(start, count), :].astype(jnp.bfloat16)
        total = total + jnp.dot(moved, block_hi, preferred_element_type=jnp.float32)
        return total + jnp.dot(moved, block_lo, preferred_element_type=jnp.float32)

    def skew(ref, pair):
        window = jnp.broadcast_to(ref[pl.ds(pair, 1), :], (rows, 3 * rows))
        return pltpu.roll(window, 2 * rows, 1, stride=1, stride_axis=0)

    def add_pair(total, pair, offset, count):
        high = skew(window_ref, pair)
        low = skew(window_lo_ref, pair)
        first = (high[:, :rows].astype(jnp.bfloat16), low[:, :rows].astype(jnp.bfloat16))
        total = add_lag(total, *first, 2 * pair, offset, count)
        second = (
            high[:, rows : 2 * rows].astype(jnp.bfloat16),
            low[:, rows : 2 * rows].astype(jnp.bfloat16),
        )
        return add_lag(total, *second, 2 * pair + 1, offset, count)

    def place(values, first):
        for row in range(values.shape[0] // width):
            for piece in range(rows // part):
                block = (first + row) * (rows // part) + piece
                out_ref[device_ref[block]] = values[
                    row * width : (row + 1) * width, piece * part : (piece + 1) * part
                ]

    quarters = 4
    quarter = lanes // quarters
    total = jnp.zeros((lanes, rows), jnp.float32)
    for index in range(quarters):
        first = index * quarter
        total = lax.fori_loop(
            index * pairs // quarters,
            (index + 1) * pairs // quarters,
            lambda pair, acc, first=first: add_pair(acc, pair, first, lanes - first),
            total,
        )
        place(total[:quarter], first // width)
        total = total[quarter:]


def causal_conv(device_of, window, incoming, width):
    window_hi = to_bf16_grid(window)
    window_lo = to_bf16_grid(window - window_hi)
    blocks, _, part = incoming.shape
    rows = window.shape[1] // 3
    lanes = blocks * part // rows * width
    return pl.pallas_call(
        lambda *refs: conv_kernel(width, *refs),
        out_shape=jax.ShapeDtypeStruct((blocks, width, part), jnp.float32),
        in_specs=[pl.BlockSpec(memory_space=pltpu.SMEM)] + [pl.BlockSpec(memory_space=pltpu.VMEM)] * 3,
        out_specs=pl.BlockSpec(memory_space=pltpu.VMEM),
        scratch_shapes=[pltpu.VMEM((2 * lanes, rows), jnp.float32)],
        cost_estimate=pl.CostEstimate(
            flops=4 * rows * rows * lanes * 2 * window.shape[0],
            bytes_accessed=window.size * 4 + incoming.size * 2 + rows * lanes * 4,
            transcendentals=0,
        ),
    )(device_of, window_hi, window_lo, incoming)


def body(query, key, value, filter_taps, conv_bias, norm_gain, pair_list):
    rows = query.shape[0]
    channels = query.shape[1]
    groups = filter_taps.shape[1]
    blocks = lax.axis_size("ctx")
    width = channels // blocks
    share = (channels // groups) // width
    holder, device_of = placement(pair_list, blocks)

    product = to_bf16_grid(key.astype(jnp.float32) * value.astype(jnp.float32))
    signal = product.astype(jnp.bfloat16)

    taps_hi = to_bf16_grid(filter_taps)
    taps_lo = filter_taps - taps_hi
    coded = jnp.repeat(jnp.stack([taps_hi.T, taps_lo.T], axis=1), share, axis=0)
    tile = 16
    outgoing = jnp.concatenate(
        [
            signal.T.reshape(blocks, width, rows),
            coded.astype(jnp.bfloat16),
            jnp.zeros((blocks, tile - width - 2, rows), jnp.bfloat16),
        ],
        axis=1,
    )
    incoming = lax.all_to_all(outgoing, "ctx", 0, 0, tiled=True)
    taps_in = incoming[:, width : width + 2, :].astype(jnp.float32)
    span = 2 * rows
    wide = blocks // 2
    my_taps = (taps_in[:, 0, :] + taps_in[:, 1, :]).reshape(wide, span)
    shifted = jnp.concatenate([jnp.zeros((1, span), jnp.float32), my_taps], axis=0)
    window = jnp.concatenate([shifted[0:-1:2], shifted[1::2], shifted[2::2]], axis=1)

    conv = causal_conv(device_of, window, incoming, width)
    conv = lax.all_to_all(conv, "ctx", 0, 0, tiled=True)
    conv = conv.transpose(2, 0, 1).reshape(rows, channels)

    long_conv = conv + conv_bias[None, :] * product
    gated = query.astype(jnp.float32) * long_conv
    squares = jnp.sum(gated * gated, axis=1)
    total_sq = jnp.sum(lax.all_gather(squares, "ch"), axis=0)
    scaling = lax.rsqrt(total_sq / (channels * lax.axis_size("ch")) + 1e-05)
    return (gated * scaling[:, None] * norm_gain[None, :]).astype(jnp.bfloat16)


def solution(mesh):
    placed = (P("ctx", "ch"), P("ctx", "ch"), P("ctx", "ch"), P("ctx", "ch"), P("ch"), P("ch"), P())
    return jax.shard_map(
        body, mesh=mesh, in_specs=placed, out_specs=P("ctx", "ch"), check_vma=False
    )
```

```python
import jax
import jax.numpy as jnp
from jax import lax
from jax.experimental import pallas as pl
from jax.experimental.pallas import tpu as pltpu
from jax.sharding import PartitionSpec as P


def placement(pair_list, blocks):
    source = pair_list[:, 0]
    target = pair_list[:, 1]
    runner = pair_list[:, 2]
    slots = lax.iota(jnp.int32, blocks)
    on_diag = source == target
    holds = on_diag[:, None] & (runner[:, None] == slots[None, :])
    holder = jnp.sum(jnp.where(holds, source[:, None], 0), axis=0)
    keeps = on_diag[:, None] & (source[:, None] == slots[None, :])
    device_of = jnp.sum(jnp.where(keeps, runner[:, None], 0), axis=0)
    return holder, device_of


def to_bf16_grid(values):
    return lax.reduce_precision(values, exponent_bits=8, mantissa_bits=7)


def conv_kernel(width, device_ref, incoming_ref, out_ref, padded_ref, window_ref, window_lo_ref):
    part = out_ref.shape[2]
    rows = window_ref.shape[1] // 3
    pairs = window_ref.shape[0]
    lanes = 2 * pairs * width
    pieces = rows // part
    for pair in range(pairs):
        for slot in range(3 * pieces):
            source = (2 * pair - 1) * pieces + slot
            for ref, line in ((window_ref, width), (window_lo_ref, width + 1)):
                if source < 0:
                    ref[pl.ds(pair, 1), pl.ds(slot * part, part)] = jnp.zeros((1, part), jnp.float32)
                else:
                    ref[pl.ds(pair, 1), pl.ds(slot * part, part)] = incoming_ref[
                        source, pl.ds(line, 1), :
                    ].astype(jnp.float32)
    padded_ref[pl.ds(0, lanes), :] = jnp.zeros((lanes, rows), jnp.float32)
    for block in range(incoming_ref.shape[0]):
        line = lanes + (block // (rows // part)) * width
        column = (block % (rows // part)) * part
        padded_ref[pl.ds(line, width), pl.ds(column, part)] = incoming_ref[
            device_ref[block], pl.ds(0, width), :
        ].astype(jnp.float32)

    def add_lag(total, block_hi, block_lo, lag, offset, count):
        start = pl.multiple_of(lanes - lag * width + offset, width)
        moved = padded_ref[pl.ds(start, count), :].astype(jnp.bfloat16)
        total = total + jnp.dot(moved, block_hi, preferred_element_type=jnp.float32)
        return total + jnp.dot(moved, block_lo, preferred_element_type=jnp.float32)

    def skew(ref, pair):
        window = jnp.broadcast_to(ref[pl.ds(pair, 1), :], (rows, 3 * rows))
        return pltpu.roll(window, 2 * rows, 1, stride=1, stride_axis=0)

    def add_pair(total, pair, offset, count):
        high = skew(window_ref, pair)
        low = skew(window_lo_ref, pair)
        first = (high[:, :rows].astype(jnp.bfloat16), low[:, :rows].astype(jnp.bfloat16))
        total = add_lag(total, *first, 2 * pair, offset, count)
        second = (
            high[:, rows : 2 * rows].astype(jnp.bfloat16),
            low[:, rows : 2 * rows].astype(jnp.bfloat16),
        )
        return add_lag(total, *second, 2 * pair + 1, offset, count)

    def place(values, first):
        for row in range(values.shape[0] // width):
            for piece in range(rows // part):
                block = (first + row) * (rows // part) + piece
                out_ref[device_ref[block]] = values[
                    row * width : (row + 1) * width, piece * part : (piece + 1) * part
                ]

    quarters = 4
    quarter = lanes // quarters
    total = jnp.zeros((lanes, rows), jnp.float32)
    for index in range(quarters):
        first = index * quarter
        total = lax.fori_loop(
            index * pairs // quarters,
            (index + 1) * pairs // quarters,
            lambda pair, acc, first=first: add_pair(acc, pair, first, lanes - first),
            total,
        )
        place(total[:quarter], first // width)
        total = total[quarter:]


def causal_conv(device_of, incoming, width):
    blocks, _, part = incoming.shape
    rows = 2 * part
    pairs = blocks * part // (2 * rows)
    lanes = 2 * pairs * width
    return pl.pallas_call(
        lambda *refs: conv_kernel(width, *refs),
        out_shape=jax.ShapeDtypeStruct((blocks, width, part), jnp.float32),
        in_specs=[pl.BlockSpec(memory_space=pltpu.SMEM), pl.BlockSpec(memory_space=pltpu.VMEM)],
        out_specs=pl.BlockSpec(memory_space=pltpu.VMEM),
        scratch_shapes=[
            pltpu.VMEM((2 * lanes, rows), jnp.float32),
            pltpu.VMEM((pairs, 3 * rows), jnp.float32),
            pltpu.VMEM((pairs, 3 * rows), jnp.float32),
        ],
        cost_estimate=pl.CostEstimate(
            flops=4 * rows * rows * lanes * 2 * pairs,
            bytes_accessed=incoming.size * 2 + rows * lanes * 4,
            transcendentals=0,
        ),
    )(device_of, incoming)


def body(query, key, value, filter_taps, conv_bias, norm_gain, pair_list):
    rows = query.shape[0]
    channels = query.shape[1]
    groups = filter_taps.shape[1]
    blocks = lax.axis_size("ctx")
    width = channels // blocks
    share = (channels // groups) // width
    holder, device_of = placement(pair_list, blocks)

    product = to_bf16_grid(key.astype(jnp.float32) * value.astype(jnp.float32))
    signal = product.astype(jnp.bfloat16)

    taps_hi = to_bf16_grid(filter_taps)
    taps_lo = filter_taps - taps_hi
    coded = jnp.repeat(jnp.stack([taps_hi.T, taps_lo.T], axis=1), share, axis=0)
    tile = 16
    outgoing = jnp.concatenate(
        [
            signal.T.reshape(blocks, width, rows),
            coded.astype(jnp.bfloat16),
            jnp.zeros((blocks, tile - width - 2, rows), jnp.bfloat16),
        ],
        axis=1,
    )
    incoming = lax.all_to_all(outgoing, "ctx", 0, 0, tiled=True)
    conv = causal_conv(device_of, incoming, width)
    conv = lax.all_to_all(conv, "ctx", 0, 0, tiled=True)
    conv = conv.transpose(2, 0, 1).reshape(rows, channels)

    long_conv = conv + conv_bias[None, :] * product
    gated = query.astype(jnp.float32) * long_conv
    squares = jnp.sum(gated * gated, axis=1)
    total_sq = jnp.sum(lax.all_gather(squares, "ch"), axis=0)
    scaling = lax.rsqrt(total_sq / (channels * lax.axis_size("ch")) + 1e-05)
    return (gated * scaling[:, None] * norm_gain[None, :]).astype(jnp.bfloat16)


def solution(mesh):
    placed = (P("ctx", "ch"), P("ctx", "ch"), P("ctx", "ch"), P("ctx", "ch"), P("ch"), P("ch"), P())
    return jax.shard_map(
        body, mesh=mesh, in_specs=placed, out_specs=P("ctx", "ch"), check_vma=False
    )
```

```python
import jax
import jax.numpy as jnp
from jax import lax
from jax.experimental import pallas as pl
from jax.experimental.pallas import tpu as pltpu
from jax.sharding import PartitionSpec as P


def placement(pair_list, blocks):
    source = pair_list[:, 0]
    target = pair_list[:, 1]
    runner = pair_list[:, 2]
    slots = lax.iota(jnp.int32, blocks)
    on_diag = source == target
    holds = on_diag[:, None] & (runner[:, None] == slots[None, :])
    holder = jnp.sum(jnp.where(holds, source[:, None], 0), axis=0)
    keeps = on_diag[:, None] & (source[:, None] == slots[None, :])
    device_of = jnp.sum(jnp.where(keeps, runner[:, None], 0), axis=0)
    return holder, device_of


def to_bf16_grid(values):
    return lax.reduce_precision(values, exponent_bits=8, mantissa_bits=7)


def conv_kernel(width, device_ref, incoming_ref, out_ref, padded_ref, window_ref, window_lo_ref, even_ref, odd_ref):
    part = out_ref.shape[2]
    rows = window_ref.shape[1] // 3
    pairs = window_ref.shape[0]
    lanes = 2 * pairs * width
    pieces = rows // part
    for pair in range(pairs):
        for slot in range(3 * pieces):
            source = (2 * pair - 1) * pieces + slot
            for ref, line in ((window_ref, width), (window_lo_ref, width + 1)):
                if source < 0:
                    ref[pl.ds(pair, 1), pl.ds(slot * part, part)] = jnp.zeros((1, part), jnp.float32)
                else:
                    ref[pl.ds(pair, 1), pl.ds(slot * part, part)] = incoming_ref[
                        source, pl.ds(line, 1), :
                    ].astype(jnp.float32)
    padded_ref[pl.ds(0, lanes), :] = jnp.zeros((lanes, rows), jnp.float32)
    for block in range(incoming_ref.shape[0]):
        line = lanes + (block // (rows // part)) * width
        column = (block % (rows // part)) * part
        padded_ref[pl.ds(line, width), pl.ds(column, part)] = incoming_ref[
            device_ref[block], pl.ds(0, width), :
        ].astype(jnp.float32)

    padded_ref[pl.ds(2 * lanes, width), :] = jnp.zeros((width, rows), jnp.float32)
    even_ref[...] = padded_ref[pl.ds(0, 2 * lanes), :].astype(jnp.bfloat16)
    odd_ref[...] = padded_ref[pl.ds(width, 2 * lanes), :].astype(jnp.bfloat16)

    def add_lag(total, block_hi, block_lo, pair, parity, offset, count):
        source = odd_ref if parity else even_ref
        start = pl.multiple_of(lanes - 2 * width * (pair + parity) + offset, 2 * width)
        moved = source[pl.ds(start, count), :]
        total = total + jnp.dot(moved, block_hi, preferred_element_type=jnp.float32)
        return total + jnp.dot(moved, block_lo, preferred_element_type=jnp.float32)

    def skew(ref, pair):
        window = jnp.broadcast_to(ref[pl.ds(pair, 1), :], (rows, 3 * rows))
        return pltpu.roll(window, 2 * rows, 1, stride=1, stride_axis=0)

    def add_pair(total, pair, offset, count):
        high = skew(window_ref, pair)
        low = skew(window_lo_ref, pair)
        first = (high[:, :rows].astype(jnp.bfloat16), low[:, :rows].astype(jnp.bfloat16))
        total = add_lag(total, *first, pair, 0, offset, count)
        second = (
            high[:, rows : 2 * rows].astype(jnp.bfloat16),
            low[:, rows : 2 * rows].astype(jnp.bfloat16),
        )
        return add_lag(total, *second, pair, 1, offset, count)

    def place(values, first):
        for row in range(values.shape[0] // width):
            for piece in range(rows // part):
                block = (first + row) * (rows // part) + piece
                out_ref[device_ref[block]] = values[
                    row * width : (row + 1) * width, piece * part : (piece + 1) * part
                ]

    quarters = 4
    quarter = lanes // quarters
    total = jnp.zeros((lanes, rows), jnp.float32)
    for index in range(quarters):
        first = index * quarter
        total = lax.fori_loop(
            index * pairs // quarters,
            (index + 1) * pairs // quarters,
            lambda pair, acc, first=first: add_pair(acc, pair, first, lanes - first),
            total,
        )
        place(total[:quarter], first // width)
        total = total[quarter:]


def causal_conv(device_of, incoming, width):
    blocks, _, part = incoming.shape
    rows = 2 * part
    pairs = blocks * part // (2 * rows)
    lanes = 2 * pairs * width
    return pl.pallas_call(
        lambda *refs: conv_kernel(width, *refs),
        out_shape=jax.ShapeDtypeStruct((blocks, width, part), jnp.float32),
        in_specs=[pl.BlockSpec(memory_space=pltpu.SMEM), pl.BlockSpec(memory_space=pltpu.VMEM)],
        out_specs=pl.BlockSpec(memory_space=pltpu.VMEM),
        scratch_shapes=[
            pltpu.VMEM((2 * lanes + width, rows), jnp.float32),
            pltpu.VMEM((pairs, 3 * rows), jnp.float32),
            pltpu.VMEM((pairs, 3 * rows), jnp.float32),
            pltpu.VMEM((2 * lanes, rows), jnp.bfloat16),
            pltpu.VMEM((2 * lanes, rows), jnp.bfloat16),
        ],
        cost_estimate=pl.CostEstimate(
            flops=4 * rows * rows * lanes * 2 * pairs,
            bytes_accessed=incoming.size * 2 + rows * lanes * 4,
            transcendentals=0,
        ),
    )(device_of, incoming)


def body(query, key, value, filter_taps, conv_bias, norm_gain, pair_list):
    rows = query.shape[0]
    channels = query.shape[1]
    groups = filter_taps.shape[1]
    blocks = lax.axis_size("ctx")
    width = channels // blocks
    share = (channels // groups) // width
    holder, device_of = placement(pair_list, blocks)

    product = to_bf16_grid(key.astype(jnp.float32) * value.astype(jnp.float32))
    signal = product.astype(jnp.bfloat16)

    taps_hi = to_bf16_grid(filter_taps)
    taps_lo = filter_taps - taps_hi
    coded = jnp.repeat(jnp.stack([taps_hi.T, taps_lo.T], axis=1), share, axis=0)
    tile = 16
    outgoing = jnp.concatenate(
        [
            signal.T.reshape(blocks, width, rows),
            coded.astype(jnp.bfloat16),
            jnp.zeros((blocks, tile - width - 2, rows), jnp.bfloat16),
        ],
        axis=1,
    )
    incoming = lax.all_to_all(outgoing, "ctx", 0, 0, tiled=True)
    conv = causal_conv(device_of, incoming, width)
    conv = lax.all_to_all(conv, "ctx", 0, 0, tiled=True)
    conv = conv.transpose(2, 0, 1).reshape(rows, channels)

    long_conv = conv + conv_bias[None, :] * product
    gated = query.astype(jnp.float32) * long_conv
    squares = jnp.sum(gated * gated, axis=1)
    total_sq = jnp.sum(lax.all_gather(squares, "ch"), axis=0)
    scaling = lax.rsqrt(total_sq / (channels * lax.axis_size("ch")) + 1e-05)
    return (gated * scaling[:, None] * norm_gain[None, :]).astype(jnp.bfloat16)


def solution(mesh):
    placed = (P("ctx", "ch"), P("ctx", "ch"), P("ctx", "ch"), P("ctx", "ch"), P("ch"), P("ch"), P())
    return jax.shard_map(
        body, mesh=mesh, in_specs=placed, out_specs=P("ctx", "ch"), check_vma=False
    )
```

```python
import jax
import jax.numpy as jnp
from jax import lax
from jax.experimental import pallas as pl
from jax.experimental.pallas import tpu as pltpu
from jax.sharding import PartitionSpec as P


def placement(pair_list, blocks):
    source = pair_list[:, 0]
    target = pair_list[:, 1]
    runner = pair_list[:, 2]
    slots = lax.iota(jnp.int32, blocks)
    on_diag = source == target
    holds = on_diag[:, None] & (runner[:, None] == slots[None, :])
    holder = jnp.sum(jnp.where(holds, source[:, None], 0), axis=0)
    keeps = on_diag[:, None] & (source[:, None] == slots[None, :])
    device_of = jnp.sum(jnp.where(keeps, runner[:, None], 0), axis=0)
    return holder, device_of


def to_bf16_grid(values):
    return lax.reduce_precision(values, exponent_bits=8, mantissa_bits=7)


def conv_kernel(width, device_ref, incoming_ref, out_ref, padded_ref, window_ref, window_lo_ref):
    part = out_ref.shape[2]
    rows = window_ref.shape[1] // 3
    pairs = window_ref.shape[0]
    lanes = 2 * pairs * width
    pieces = rows // part
    for pair in range(pairs):
        for slot in range(3 * pieces):
            source = (2 * pair - 1) * pieces + slot
            for ref, line in ((window_ref, width), (window_lo_ref, width + 1)):
                if source < 0:
                    ref[pl.ds(pair, 1), pl.ds(slot * part, part)] = jnp.zeros((1, part), jnp.float32)
                else:
                    ref[pl.ds(pair, 1), pl.ds(slot * part, part)] = incoming_ref[
                        source, pl.ds(line, 1), :
                    ].astype(jnp.float32)
    padded_ref[pl.ds(0, lanes), :] = jnp.zeros((lanes, rows), jnp.float32)
    for block in range(incoming_ref.shape[0]):
        line = lanes + (block // (rows // part)) * width
        column = (block % (rows // part)) * part
        padded_ref[pl.ds(line, width), pl.ds(column, part)] = incoming_ref[
            device_ref[block], pl.ds(0, width), :
        ].astype(jnp.float32)

    def moved(lag, offset, count):
        start = pl.multiple_of(lanes - lag * width + offset, width)
        return padded_ref[pl.ds(start, count), :].astype(jnp.bfloat16)

    def skew(ref, pair):
        window = jnp.broadcast_to(ref[pl.ds(pair, 1), :], (rows, 3 * rows))
        return pltpu.roll(window, 2 * rows, 1, stride=1, stride_axis=0)

    def add_pair(total, pair, offset, count):
        high = skew(window_ref, pair)
        low = skew(window_lo_ref, pair)
        blocks = jnp.concatenate(
            [high[:, :rows], low[:, :rows], high[:, rows : 2 * rows], low[:, rows : 2 * rows]], axis=0
        ).astype(jnp.bfloat16)
        first = moved(2 * pair, offset, count)
        second = moved(2 * pair + 1, offset, count)
        inputs = jnp.concatenate([first, first, second, second], axis=1)
        return total + jnp.dot(inputs, blocks, preferred_element_type=jnp.float32)

    def place(values, first):
        for row in range(values.shape[0] // width):
            for piece in range(rows // part):
                block = (first + row) * (rows // part) + piece
                out_ref[device_ref[block]] = values[
                    row * width : (row + 1) * width, piece * part : (piece + 1) * part
                ]

    quarters = 4
    quarter = lanes // quarters
    total = jnp.zeros((lanes, rows), jnp.float32)
    for index in range(quarters):
        first = index * quarter
        total = lax.fori_loop(
            index * pairs // quarters,
            (index + 1) * pairs // quarters,
            lambda pair, acc, first=first: add_pair(acc, pair, first, lanes - first),
            total,
        )
        place(total[:quarter], first // width)
        total = total[quarter:]


def causal_conv(device_of, incoming, width):
    blocks, _, part = incoming.shape
    rows = 2 * part
    pairs = blocks * part // (2 * rows)
    lanes = 2 * pairs * width
    return pl.pallas_call(
        lambda *refs: conv_kernel(width, *refs),
        out_shape=jax.ShapeDtypeStruct((blocks, width, part), jnp.float32),
        in_specs=[pl.BlockSpec(memory_space=pltpu.SMEM), pl.BlockSpec(memory_space=pltpu.VMEM)],
        out_specs=pl.BlockSpec(memory_space=pltpu.VMEM),
        scratch_shapes=[
            pltpu.VMEM((2 * lanes, rows), jnp.float32),
            pltpu.VMEM((pairs, 3 * rows), jnp.float32),
            pltpu.VMEM((pairs, 3 * rows), jnp.float32),
        ],
        cost_estimate=pl.CostEstimate(
            flops=4 * rows * rows * lanes * 2 * pairs,
            bytes_accessed=incoming.size * 2 + rows * lanes * 4,
            transcendentals=0,
        ),
    )(device_of, incoming)


def body(query, key, value, filter_taps, conv_bias, norm_gain, pair_list):
    rows = query.shape[0]
    channels = query.shape[1]
    groups = filter_taps.shape[1]
    blocks = lax.axis_size("ctx")
    width = channels // blocks
    share = (channels // groups) // width
    holder, device_of = placement(pair_list, blocks)

    product = to_bf16_grid(key.astype(jnp.float32) * value.astype(jnp.float32))
    signal = product.astype(jnp.bfloat16)

    taps_hi = to_bf16_grid(filter_taps)
    taps_lo = filter_taps - taps_hi
    coded = jnp.repeat(jnp.stack([taps_hi.T, taps_lo.T], axis=1), share, axis=0)
    tile = 16
    outgoing = jnp.concatenate(
        [
            signal.T.reshape(blocks, width, rows),
            coded.astype(jnp.bfloat16),
            jnp.zeros((blocks, tile - width - 2, rows), jnp.bfloat16),
        ],
        axis=1,
    )
    incoming = lax.all_to_all(outgoing, "ctx", 0, 0, tiled=True)
    conv = causal_conv(device_of, incoming, width)
    conv = lax.all_to_all(conv, "ctx", 0, 0, tiled=True)
    conv = conv.transpose(2, 0, 1).reshape(rows, channels)

    long_conv = conv + conv_bias[None, :] * product
    gated = query.astype(jnp.float32) * long_conv
    squares = jnp.sum(gated * gated, axis=1)
    total_sq = jnp.sum(lax.all_gather(squares, "ch"), axis=0)
    scaling = lax.rsqrt(total_sq / (channels * lax.axis_size("ch")) + 1e-05)
    return (gated * scaling[:, None] * norm_gain[None, :]).astype(jnp.bfloat16)


def solution(mesh):
    placed = (P("ctx", "ch"), P("ctx", "ch"), P("ctx", "ch"), P("ctx", "ch"), P("ch"), P("ch"), P())
    return jax.shard_map(
        body, mesh=mesh, in_specs=placed, out_specs=P("ctx", "ch"), check_vma=False
    )
```

```python
import jax
import jax.numpy as jnp
from jax import lax
from jax.experimental import pallas as pl
from jax.experimental.pallas import tpu as pltpu
from jax.sharding import PartitionSpec as P


def placement(pair_list, blocks):
    source = pair_list[:, 0]
    target = pair_list[:, 1]
    runner = pair_list[:, 2]
    slots = lax.iota(jnp.int32, blocks)
    on_diag = source == target
    holds = on_diag[:, None] & (runner[:, None] == slots[None, :])
    holder = jnp.sum(jnp.where(holds, source[:, None], 0), axis=0)
    keeps = on_diag[:, None] & (source[:, None] == slots[None, :])
    device_of = jnp.sum(jnp.where(keeps, runner[:, None], 0), axis=0)
    return holder, device_of


def to_bf16_grid(values):
    return lax.reduce_precision(values, exponent_bits=8, mantissa_bits=7)


def conv_kernel(width, device_ref, incoming_ref, out_ref, padded_ref):
    part = out_ref.shape[2]
    rows = 2 * part
    pairs = incoming_ref.shape[0] * part // (2 * rows)
    lanes = 2 * pairs * width
    pieces = rows // part
    padded_ref[pl.ds(0, lanes), :] = jnp.zeros((lanes, rows), jnp.float32)
    for block in range(incoming_ref.shape[0]):
        line = lanes + (block // (rows // part)) * width
        column = (block % (rows // part)) * part
        padded_ref[pl.ds(line, width), pl.ds(column, part)] = incoming_ref[
            device_ref[block], pl.ds(0, width), :
        ].astype(jnp.float32)

    def add_lag(total, block_hi, block_lo, lag, offset, count):
        start = pl.multiple_of(lanes - lag * width + offset, width)
        moved = padded_ref[pl.ds(start, count), :].astype(jnp.bfloat16)
        total = total + jnp.dot(moved, block_hi, preferred_element_type=jnp.float32)
        return total + jnp.dot(moved, block_lo, preferred_element_type=jnp.float32)

    def skew(line, pair):
        columns = []
        for slot in range(3 * pieces):
            source = (2 * pair - 1) * pieces + slot
            taps = incoming_ref[jnp.maximum(source, 0), pl.ds(line, 1), :].astype(jnp.float32)
            taps = jnp.where(source >= 0, taps, 0.0)
            columns.append(jnp.broadcast_to(taps, (rows, part)))
        window = jnp.concatenate(columns, axis=1)
        return pltpu.roll(window, 2 * rows, 1, stride=1, stride_axis=0)

    def add_pair(total, pair, offset, count):
        high = skew(width, pair)
        low = skew(width + 1, pair)
        first = (high[:, :rows].astype(jnp.bfloat16), low[:, :rows].astype(jnp.bfloat16))
        total = add_lag(total, *first, 2 * pair, offset, count)
        second = (
            high[:, rows : 2 * rows].astype(jnp.bfloat16),
            low[:, rows : 2 * rows].astype(jnp.bfloat16),
        )
        return add_lag(total, *second, 2 * pair + 1, offset, count)

    def place(values, first):
        for row in range(values.shape[0] // width):
            for piece in range(rows // part):
                block = (first + row) * (rows // part) + piece
                out_ref[device_ref[block]] = values[
                    row * width : (row + 1) * width, piece * part : (piece + 1) * part
                ]

    quarters = 4
    quarter = lanes // quarters
    total = jnp.zeros((lanes, rows), jnp.float32)
    for index in range(quarters):
        first = index * quarter
        total = lax.fori_loop(
            index * pairs // quarters,
            (index + 1) * pairs // quarters,
            lambda pair, acc, first=first: add_pair(acc, pair, first, lanes - first),
            total,
        )
        place(total[:quarter], first // width)
        total = total[quarter:]


def causal_conv(device_of, incoming, width):
    blocks, _, part = incoming.shape
    rows = 2 * part
    pairs = blocks * part // (2 * rows)
    lanes = 2 * pairs * width
    return pl.pallas_call(
        lambda *refs: conv_kernel(width, *refs),
        out_shape=jax.ShapeDtypeStruct((blocks, width, part), jnp.float32),
        in_specs=[pl.BlockSpec(memory_space=pltpu.SMEM), pl.BlockSpec(memory_space=pltpu.VMEM)],
        out_specs=pl.BlockSpec(memory_space=pltpu.VMEM),
        scratch_shapes=[
            pltpu.VMEM((2 * lanes, rows), jnp.float32),
        ],
        cost_estimate=pl.CostEstimate(
            flops=4 * rows * rows * lanes * 2 * pairs,
            bytes_accessed=incoming.size * 2 + rows * lanes * 4,
            transcendentals=0,
        ),
    )(device_of, incoming)


def body(query, key, value, filter_taps, conv_bias, norm_gain, pair_list):
    rows = query.shape[0]
    channels = query.shape[1]
    groups = filter_taps.shape[1]
    blocks = lax.axis_size("ctx")
    width = channels // blocks
    share = (channels // groups) // width
    holder, device_of = placement(pair_list, blocks)

    product = to_bf16_grid(key.astype(jnp.float32) * value.astype(jnp.float32))
    signal = product.astype(jnp.bfloat16)

    taps_hi = to_bf16_grid(filter_taps)
    taps_lo = filter_taps - taps_hi
    coded = jnp.repeat(jnp.stack([taps_hi.T, taps_lo.T], axis=1), share, axis=0)
    tile = 16
    outgoing = jnp.concatenate(
        [
            signal.T.reshape(blocks, width, rows),
            coded.astype(jnp.bfloat16),
            jnp.zeros((blocks, tile - width - 2, rows), jnp.bfloat16),
        ],
        axis=1,
    )
    incoming = lax.all_to_all(outgoing, "ctx", 0, 0, tiled=True)
    conv = causal_conv(device_of, incoming, width)
    conv = lax.all_to_all(conv, "ctx", 0, 0, tiled=True)
    conv = conv.transpose(2, 0, 1).reshape(rows, channels)

    long_conv = conv + conv_bias[None, :] * product
    gated = query.astype(jnp.float32) * long_conv
    squares = jnp.sum(gated * gated, axis=1)
    total_sq = jnp.sum(lax.all_gather(squares, "ch"), axis=0)
    scaling = lax.rsqrt(total_sq / (channels * lax.axis_size("ch")) + 1e-05)
    return (gated * scaling[:, None] * norm_gain[None, :]).astype(jnp.bfloat16)


def solution(mesh):
    placed = (P("ctx", "ch"), P("ctx", "ch"), P("ctx", "ch"), P("ctx", "ch"), P("ch"), P("ch"), P())
    return jax.shard_map(
        body, mesh=mesh, in_specs=placed, out_specs=P("ctx", "ch"), check_vma=False
    )
```

```python
import jax
import jax.numpy as jnp
from jax import lax
from jax.experimental import pallas as pl
from jax.experimental.pallas import tpu as pltpu
from jax.sharding import PartitionSpec as P


def placement(pair_list, blocks):
    source = pair_list[:, 0]
    target = pair_list[:, 1]
    runner = pair_list[:, 2]
    slots = lax.iota(jnp.int32, blocks)
    on_diag = source == target
    holds = on_diag[:, None] & (runner[:, None] == slots[None, :])
    holder = jnp.sum(jnp.where(holds, source[:, None], 0), axis=0)
    keeps = on_diag[:, None] & (source[:, None] == slots[None, :])
    device_of = jnp.sum(jnp.where(keeps, runner[:, None], 0), axis=0)
    return holder, device_of


def to_bf16_grid(values):
    return lax.reduce_precision(values, exponent_bits=8, mantissa_bits=7)


def conv_kernel(width, device_ref, incoming_ref, out_ref, padded_ref, window_ref, window_lo_ref):
    part = out_ref.shape[2]
    rows = window_ref.shape[1] // 3
    pairs = window_ref.shape[0]
    lanes = 2 * pairs * width
    pieces = rows // part
    for pair in range(pairs):
        for slot in range(3 * pieces):
            source = (2 * pair - 1) * pieces + slot
            for ref, line in ((window_ref, width), (window_lo_ref, width + 1)):
                if source < 0:
                    ref[pl.ds(pair, 1), pl.ds(slot * part, part)] = jnp.zeros((1, part), jnp.float32)
                else:
                    ref[pl.ds(pair, 1), pl.ds(slot * part, part)] = incoming_ref[
                        source, pl.ds(line, 1), :
                    ].astype(jnp.float32)
    padded_ref[pl.ds(0, lanes), :] = jnp.zeros((lanes, rows), jnp.float32)
    for block in range(incoming_ref.shape[0]):
        line = lanes + (block // (rows // part)) * width
        column = (block % (rows // part)) * part
        padded_ref[pl.ds(line, width), pl.ds(column, part)] = incoming_ref[
            device_ref[block], pl.ds(0, width), :
        ].astype(jnp.float32)

    def add_lag(total, block_hi, block_lo, lag, offset, count):
        start = pl.multiple_of(lanes - lag * width + offset, width)
        moved = padded_ref[pl.ds(start, count), :].astype(jnp.bfloat16)
        total = total + jnp.dot(moved, block_hi, preferred_element_type=jnp.float32)
        return total + jnp.dot(moved, block_lo, preferred_element_type=jnp.float32)

    def skew(ref, pair):
        window = jnp.broadcast_to(ref[pl.ds(pair, 1), :], (rows, 3 * rows))
        return pltpu.roll(window, 2 * rows, 1, stride=1, stride_axis=0)

    def add_pair(total, pair, offset, count):
        high = skew(window_ref, pair)
        low = skew(window_lo_ref, pair)
        first = (high[:, :rows].astype(jnp.bfloat16), low[:, :rows].astype(jnp.bfloat16))
        total = add_lag(total, *first, 2 * pair, offset, count)
        second = (
            high[:, rows : 2 * rows].astype(jnp.bfloat16),
            low[:, rows : 2 * rows].astype(jnp.bfloat16),
        )
        return add_lag(total, *second, 2 * pair + 1, offset, count)

    def place(values, first):
        for row in range(values.shape[0] // width):
            for piece in range(rows // part):
                block = (first + row) * (rows // part) + piece
                out_ref[device_ref[block]] = values[
                    row * width : (row + 1) * width, piece * part : (piece + 1) * part
                ]

    quarters = 4
    quarter = lanes // quarters
    total = jnp.zeros((lanes, rows), jnp.float32)
    for index in range(quarters):
        first = index * quarter
        total = lax.fori_loop(
            index * pairs // quarters,
            (index + 1) * pairs // quarters,
            lambda pair, acc, first=first: add_pair(acc, pair, first, lanes - first),
            total,
            unroll=True,
        )
        place(total[:quarter], first // width)
        total = total[quarter:]


def causal_conv(device_of, incoming, width):
    blocks, _, part = incoming.shape
    rows = 2 * part
    pairs = blocks * part // (2 * rows)
    lanes = 2 * pairs * width
    return pl.pallas_call(
        lambda *refs: conv_kernel(width, *refs),
        out_shape=jax.ShapeDtypeStruct((blocks, width, part), jnp.float32),
        in_specs=[pl.BlockSpec(memory_space=pltpu.SMEM), pl.BlockSpec(memory_space=pltpu.VMEM)],
        out_specs=pl.BlockSpec(memory_space=pltpu.VMEM),
        scratch_shapes=[
            pltpu.VMEM((2 * lanes, rows), jnp.float32),
            pltpu.VMEM((pairs, 3 * rows), jnp.float32),
            pltpu.VMEM((pairs, 3 * rows), jnp.float32),
        ],
        cost_estimate=pl.CostEstimate(
            flops=4 * rows * rows * lanes * 2 * pairs,
            bytes_accessed=incoming.size * 2 + rows * lanes * 4,
            transcendentals=0,
        ),
    )(device_of, incoming)


def body(query, key, value, filter_taps, conv_bias, norm_gain, pair_list):
    rows = query.shape[0]
    channels = query.shape[1]
    groups = filter_taps.shape[1]
    blocks = lax.axis_size("ctx")
    width = channels // blocks
    share = (channels // groups) // width
    holder, device_of = placement(pair_list, blocks)

    product = to_bf16_grid(key.astype(jnp.float32) * value.astype(jnp.float32))
    signal = product.astype(jnp.bfloat16)

    taps_hi = to_bf16_grid(filter_taps)
    taps_lo = filter_taps - taps_hi
    coded = jnp.repeat(jnp.stack([taps_hi.T, taps_lo.T], axis=1), share, axis=0)
    tile = 16
    outgoing = jnp.concatenate(
        [
            signal.T.reshape(blocks, width, rows),
            coded.astype(jnp.bfloat16),
            jnp.zeros((blocks, tile - width - 2, rows), jnp.bfloat16),
        ],
        axis=1,
    )
    incoming = lax.all_to_all(outgoing, "ctx", 0, 0, tiled=True)
    conv = causal_conv(device_of, incoming, width)
    conv = lax.all_to_all(conv, "ctx", 0, 0, tiled=True)
    conv = conv.transpose(2, 0, 1).reshape(rows, channels)

    long_conv = conv + conv_bias[None, :] * product
    gated = query.astype(jnp.float32) * long_conv
    squares = jnp.sum(gated * gated, axis=1)
    total_sq = jnp.sum(lax.all_gather(squares, "ch"), axis=0)
    scaling = lax.rsqrt(total_sq / (channels * lax.axis_size("ch")) + 1e-05)
    return (gated * scaling[:, None] * norm_gain[None, :]).astype(jnp.bfloat16)


def solution(mesh):
    placed = (P("ctx", "ch"), P("ctx", "ch"), P("ctx", "ch"), P("ctx", "ch"), P("ch"), P("ch"), P())
    return jax.shard_map(
        body, mesh=mesh, in_specs=placed, out_specs=P("ctx", "ch"), check_vma=False
    )
```

```python
import jax
import jax.numpy as jnp
from jax import lax
from jax.experimental import pallas as pl
from jax.experimental.pallas import tpu as pltpu
from jax.sharding import PartitionSpec as P


def placement(pair_list, blocks):
    source = pair_list[:, 0]
    target = pair_list[:, 1]
    runner = pair_list[:, 2]
    slots = lax.iota(jnp.int32, blocks)
    on_diag = source == target
    holds = on_diag[:, None] & (runner[:, None] == slots[None, :])
    holder = jnp.sum(jnp.where(holds, source[:, None], 0), axis=0)
    keeps = on_diag[:, None] & (source[:, None] == slots[None, :])
    device_of = jnp.sum(jnp.where(keeps, runner[:, None], 0), axis=0)
    return holder, device_of


def to_bf16_grid(values):
    return lax.reduce_precision(values, exponent_bits=8, mantissa_bits=7)


def conv_kernel(width, device_ref, incoming_ref, out_ref, padded_ref, window_ref, window_lo_ref):
    part = out_ref.shape[2]
    rows = window_ref.shape[1] // 3
    pairs = window_ref.shape[0]
    lanes = 2 * pairs * width
    pieces = rows // part
    for pair in range(pairs):
        for slot in range(3 * pieces):
            source = (2 * pair - 1) * pieces + slot
            for ref, line in ((window_ref, width), (window_lo_ref, width + 1)):
                if source < 0:
                    ref[pl.ds(pair, 1), pl.ds(slot * part, part)] = jnp.zeros((1, part), jnp.float32)
                else:
                    ref[pl.ds(pair, 1), pl.ds(slot * part, part)] = incoming_ref[
                        source, pl.ds(line, 1), :
                    ].astype(jnp.float32)
    padded_ref[pl.ds(0, lanes), :] = jnp.zeros((lanes, rows), jnp.float32)
    for block in range(incoming_ref.shape[0]):
        line = lanes + (block // (rows // part)) * width
        column = (block % (rows // part)) * part
        padded_ref[pl.ds(line, width), pl.ds(column, part)] = incoming_ref[
            device_ref[block], pl.ds(0, width), :
        ].astype(jnp.float32)

    def add_lag(total, block_hi, block_lo, lag, offset, count):
        start = pl.multiple_of(lanes - lag * width + offset, width)
        moved = padded_ref[pl.ds(start, count), :].astype(jnp.bfloat16)
        total = total + jnp.dot(moved, block_hi, preferred_element_type=jnp.float32)
        return total + jnp.dot(moved, block_lo, preferred_element_type=jnp.float32)

    def skew(ref, pair):
        window = jnp.broadcast_to(ref[pl.ds(pair, 1), :], (rows, 3 * rows))
        return pltpu.roll(window, 2 * rows, 1, stride=1, stride_axis=0)

    def add_pair(total, pair, offset, count):
        high = skew(window_ref, pair)
        low = skew(window_lo_ref, pair)
        first = (high[:, :rows].astype(jnp.bfloat16), low[:, :rows].astype(jnp.bfloat16))
        total = add_lag(total, *first, 2 * pair, offset, count)
        second = (
            high[:, rows : 2 * rows].astype(jnp.bfloat16),
            low[:, rows : 2 * rows].astype(jnp.bfloat16),
        )
        return add_lag(total, *second, 2 * pair + 1, offset, count)

    def place(values, first):
        for row in range(values.shape[0] // width):
            for piece in range(rows // part):
                block = (first + row) * (rows // part) + piece
                out_ref[device_ref[block]] = values[
                    row * width : (row + 1) * width, piece * part : (piece + 1) * part
                ]

    step = 2 * width
    total = jnp.zeros((lanes, rows), jnp.float32)
    for pair in range(pairs):
        first = pair * step
        total = add_pair(total, pair, first, lanes - first)
        place(total[:step], first // width)
        total = total[step:]


def causal_conv(device_of, incoming, width):
    blocks, _, part = incoming.shape
    rows = 2 * part
    pairs = blocks * part // (2 * rows)
    lanes = 2 * pairs * width
    return pl.pallas_call(
        lambda *refs: conv_kernel(width, *refs),
        out_shape=jax.ShapeDtypeStruct((blocks, width, part), jnp.float32),
        in_specs=[pl.BlockSpec(memory_space=pltpu.SMEM), pl.BlockSpec(memory_space=pltpu.VMEM)],
        out_specs=pl.BlockSpec(memory_space=pltpu.VMEM),
        scratch_shapes=[
            pltpu.VMEM((2 * lanes, rows), jnp.float32),
            pltpu.VMEM((pairs, 3 * rows), jnp.float32),
            pltpu.VMEM((pairs, 3 * rows), jnp.float32),
        ],
        cost_estimate=pl.CostEstimate(
            flops=4 * rows * rows * lanes * 2 * pairs,
            bytes_accessed=incoming.size * 2 + rows * lanes * 4,
            transcendentals=0,
        ),
    )(device_of, incoming)


def body(query, key, value, filter_taps, conv_bias, norm_gain, pair_list):
    rows = query.shape[0]
    channels = query.shape[1]
    groups = filter_taps.shape[1]
    blocks = lax.axis_size("ctx")
    width = channels // blocks
    share = (channels // groups) // width
    holder, device_of = placement(pair_list, blocks)

    product = to_bf16_grid(key.astype(jnp.float32) * value.astype(jnp.float32))
    signal = product.astype(jnp.bfloat16)

    taps_hi = to_bf16_grid(filter_taps)
    taps_lo = filter_taps - taps_hi
    coded = jnp.repeat(jnp.stack([taps_hi.T, taps_lo.T], axis=1), share, axis=0)
    tile = 16
    outgoing = jnp.concatenate(
        [
            signal.T.reshape(blocks, width, rows),
            coded.astype(jnp.bfloat16),
            jnp.zeros((blocks, tile - width - 2, rows), jnp.bfloat16),
        ],
        axis=1,
    )
    incoming = lax.all_to_all(outgoing, "ctx", 0, 0, tiled=True)
    conv = causal_conv(device_of, incoming, width)
    conv = lax.all_to_all(conv, "ctx", 0, 0, tiled=True)
    conv = conv.transpose(2, 0, 1).reshape(rows, channels)

    long_conv = conv + conv_bias[None, :] * product
    gated = query.astype(jnp.float32) * long_conv
    squares = jnp.sum(gated * gated, axis=1)
    total_sq = jnp.sum(lax.all_gather(squares, "ch"), axis=0)
    scaling = lax.rsqrt(total_sq / (channels * lax.axis_size("ch")) + 1e-05)
    return (gated * scaling[:, None] * norm_gain[None, :]).astype(jnp.bfloat16)


def solution(mesh):
    placed = (P("ctx", "ch"), P("ctx", "ch"), P("ctx", "ch"), P("ctx", "ch"), P("ch"), P("ch"), P())
    return jax.shard_map(
        body, mesh=mesh, in_specs=placed, out_specs=P("ctx", "ch"), check_vma=False
    )
```

```python
import jax
import jax.numpy as jnp
from jax import lax
from jax.experimental import pallas as pl
from jax.experimental.pallas import tpu as pltpu
from jax.sharding import PartitionSpec as P


def placement(pair_list, blocks):
    source = pair_list[:, 0]
    target = pair_list[:, 1]
    runner = pair_list[:, 2]
    slots = lax.iota(jnp.int32, blocks)
    on_diag = source == target
    holds = on_diag[:, None] & (runner[:, None] == slots[None, :])
    holder = jnp.sum(jnp.where(holds, source[:, None], 0), axis=0)
    keeps = on_diag[:, None] & (source[:, None] == slots[None, :])
    device_of = jnp.sum(jnp.where(keeps, runner[:, None], 0), axis=0)
    return holder, device_of


def to_bf16_grid(values):
    return lax.reduce_precision(values, exponent_bits=8, mantissa_bits=7)


def conv_kernel(width, device_ref, incoming_ref, out_ref, padded_ref, window_ref, window_lo_ref):
    part = out_ref.shape[2]
    rows = window_ref.shape[1] // 3
    pairs = window_ref.shape[0]
    lanes = 2 * pairs * width
    pieces = rows // part
    for pair in range(pairs):
        for slot in range(3 * pieces):
            source = (2 * pair - 1) * pieces + slot
            for ref, line in ((window_ref, width), (window_lo_ref, width + 1)):
                if source < 0:
                    ref[pl.ds(pair, 1), pl.ds(slot * part, part)] = jnp.zeros((1, part), jnp.float32)
                else:
                    ref[pl.ds(pair, 1), pl.ds(slot * part, part)] = incoming_ref[
                        source, pl.ds(line, 1), :
                    ].astype(jnp.float32)
    padded_ref[pl.ds(0, lanes), :] = jnp.zeros((lanes, rows), jnp.float32)
    for block in range(incoming_ref.shape[0]):
        line = lanes + (block // (rows // part)) * width
        column = (block % (rows // part)) * part
        padded_ref[pl.ds(line, width), pl.ds(column, part)] = incoming_ref[
            device_ref[block], pl.ds(0, width), :
        ].astype(jnp.float32)

    def moved(lag, offset, count):
        start = pl.multiple_of(lanes - lag * width + offset, width)
        return padded_ref[pl.ds(start, count), :].astype(jnp.bfloat16)

    def skew(ref, pair):
        window = jnp.broadcast_to(ref[pl.ds(pair, 1), :], (rows, 3 * rows))
        return pltpu.roll(window, 2 * rows, 1, stride=1, stride_axis=0)

    def add_pair(total, pair, offset, count):
        high = skew(window_ref, pair)
        low = skew(window_lo_ref, pair)
        blocks = jnp.concatenate(
            [high[:, :rows], low[:, :rows], high[:, rows : 2 * rows], low[:, rows : 2 * rows]], axis=0
        ).astype(jnp.bfloat16)
        first = moved(2 * pair, offset, count)
        second = moved(2 * pair + 1, offset, count)
        inputs = jnp.concatenate([first, first, second, second], axis=1)
        return total + jnp.dot(inputs, blocks, preferred_element_type=jnp.float32)

    def place(values, first):
        for row in range(values.shape[0] // width):
            for piece in range(rows // part):
                block = (first + row) * (rows // part) + piece
                out_ref[device_ref[block]] = values[
                    row * width : (row + 1) * width, piece * part : (piece + 1) * part
                ]

    step = 2 * width
    total = jnp.zeros((lanes, rows), jnp.float32)
    for pair in range(pairs):
        first = pair * step
        total = add_pair(total, pair, first, lanes - first)
        place(total[:step], first // width)
        total = total[step:]


def causal_conv(device_of, incoming, width):
    blocks, _, part = incoming.shape
    rows = 2 * part
    pairs = blocks * part // (2 * rows)
    lanes = 2 * pairs * width
    return pl.pallas_call(
        lambda *refs: conv_kernel(width, *refs),
        out_shape=jax.ShapeDtypeStruct((blocks, width, part), jnp.float32),
        in_specs=[pl.BlockSpec(memory_space=pltpu.SMEM), pl.BlockSpec(memory_space=pltpu.VMEM)],
        out_specs=pl.BlockSpec(memory_space=pltpu.VMEM),
        scratch_shapes=[
            pltpu.VMEM((2 * lanes, rows), jnp.float32),
            pltpu.VMEM((pairs, 3 * rows), jnp.float32),
            pltpu.VMEM((pairs, 3 * rows), jnp.float32),
        ],
        cost_estimate=pl.CostEstimate(
            flops=4 * rows * rows * lanes * 2 * pairs,
            bytes_accessed=incoming.size * 2 + rows * lanes * 4,
            transcendentals=0,
        ),
    )(device_of, incoming)


def body(query, key, value, filter_taps, conv_bias, norm_gain, pair_list):
    rows = query.shape[0]
    channels = query.shape[1]
    groups = filter_taps.shape[1]
    blocks = lax.axis_size("ctx")
    width = channels // blocks
    share = (channels // groups) // width
    holder, device_of = placement(pair_list, blocks)

    product = to_bf16_grid(key.astype(jnp.float32) * value.astype(jnp.float32))
    signal = product.astype(jnp.bfloat16)

    taps_hi = to_bf16_grid(filter_taps)
    taps_lo = filter_taps - taps_hi
    coded = jnp.repeat(jnp.stack([taps_hi.T, taps_lo.T], axis=1), share, axis=0)
    tile = 16
    outgoing = jnp.concatenate(
        [
            signal.T.reshape(blocks, width, rows),
            coded.astype(jnp.bfloat16),
            jnp.zeros((blocks, tile - width - 2, rows), jnp.bfloat16),
        ],
        axis=1,
    )
    incoming = lax.all_to_all(outgoing, "ctx", 0, 0, tiled=True)
    conv = causal_conv(device_of, incoming, width)
    conv = lax.all_to_all(conv, "ctx", 0, 0, tiled=True)
    conv = conv.transpose(2, 0, 1).reshape(rows, channels)

    long_conv = conv + conv_bias[None, :] * product
    gated = query.astype(jnp.float32) * long_conv
    squares = jnp.sum(gated * gated, axis=1)
    total_sq = jnp.sum(lax.all_gather(squares, "ch"), axis=0)
    scaling = lax.rsqrt(total_sq / (channels * lax.axis_size("ch")) + 1e-05)
    return (gated * scaling[:, None] * norm_gain[None, :]).astype(jnp.bfloat16)


def solution(mesh):
    placed = (P("ctx", "ch"), P("ctx", "ch"), P("ctx", "ch"), P("ctx", "ch"), P("ch"), P("ch"), P())
    return jax.shard_map(
        body, mesh=mesh, in_specs=placed, out_specs=P("ctx", "ch"), check_vma=False
    )
```
